128 devices in a mesh: grp: 4 (over z), dev: 32 (over x, y, core).
Axes of the slice: x: 4, y: 4, z: 4, core: 2. Of those that a mesh axis runs over, the one named last changes fastest.
Arguments:
- rhs: float32 [8192, 64, 128], P(('grp', 'dev')), may hold values from -6 to 6
- jacobian: bfloat16 [8192, 7, 128, 128], P(('grp', 'dev'))
- columns: int32 [8192, 7], P(('grp', 'dev')), may hold values from 0 to 95, as said below
- send_tiles: int32 [128, 4, 8], P(('grp', 'dev')), may hold values from 0 to 63
- smoother: bfloat16 [8192, 128, 128], P(('grp', 'dev'))
- restriction: bfloat16 [8192, 128, 128], P(('grp', 'dev')), may hold values from -0.25 to 0.25
- coarse_inverse: bfloat16 [32, 32, 2, 128, 128], P('dev')
- owner: int32 [1024, 1], replicated, may hold values from 0 to 31; in each aligned block of 32 rows (0 to 31, 32 to 63, ...) at most 2 rows name the same one
Outputs:
- correction: float32 [8192, 64, 128], P(('grp', 'dev'))
The draws below stay inside these ranges and needn't reach their ends.
Inputs may be any that keep to these rules, and one draw needn't show every extreme that they name: columns[n, 0] is the local index t of tile n itself; columns[n, 1] and columns[n, 2] are below 64; columns[n, 3 + j] lies in 64 + j * 8 to 64 + (j + 1) * 8 - 1. In each aligned block of 32 rows (the coarse blocks of one domain position) no owner is named more than 2 times.
All inputs are finite; a program needn't handle non-finite values.
Results may differ from the reference program's by a relative error of at most 0.0035.
Values may be sent and summed in bfloat16 or wider, within the bound.
No kernel may reach another device: no remote copies, remote signals or barrier semaphores. Data moves between devices by JAX's collectives and lax.ppermute only.
A program may use at most 128 MiB of HBM per device.

```python
import math
import jax
import jax.numpy as jnp
import numpy as np
from jax import lax

R = 128
K = 7
AGG = 2
SWEEPS = 3
NRHS = 64
TPD = 64
SUBS = 4
DOMS = 32
HB = 8
CPD = 32
CAP = 2
COARSE = 1024
TILES = 8192


def draw_jacobian(key, part):
    shape = (TILES, K, R, R)
    base = jax.random.normal(key, shape, jnp.float32)
    first = (jnp.arange(K) == 0).astype(jnp.float32)
    scale = (0.15 + 0.45 * first) / math.sqrt(R)
    diagonal = 2.0 * first[:, None, None] * jnp.eye(R, dtype=jnp.float32)[None]
    return (base * scale[None, :, None, None] + diagonal[None]).astype(jnp.bfloat16)


def draw_columns(key, part):
    key_local, key_halo = jax.random.split(jax.random.fold_in(key, 11))
    local = jax.random.randint(key_local, (TILES, 2), 0, TPD)
    halo = jax.random.randint(key_halo, (TILES, 4), 0, HB) + TPD + HB * jnp.arange(4, dtype=jnp.int32)[None, :]
    itself = jnp.arange(TILES, dtype=jnp.int32) % TPD
    return jnp.concatenate([itself[:, None], local, halo], axis=1).astype(jnp.int32)


def draw_smoother(key, part):
    shape = (TILES, R, R)
    base = jax.random.normal(key, shape, jnp.float32)
    return (0.3 * jnp.eye(R, dtype=jnp.float32)[None] + base * (0.12 / math.sqrt(R))).astype(jnp.bfloat16)


def draw_coarse_inverse(key, part):
    shape = (DOMS, DOMS, CAP, R, R)
    base = jax.random.normal(key, shape, jnp.float32)
    return (0.5 * jnp.eye(R, dtype=jnp.float32) + base * (0.2 / math.sqrt(R))).astype(jnp.bfloat16)


def with_ends(drawn, stream_key, least, high):
    dims = drawn.shape
    spot = [jax.random.randint(jax.random.fold_in(stream_key, axis), (), 0, dims[axis]) for axis in range(len(dims))]
    drawn = drawn.at[tuple(spot)].set(least)
    longest = dims.index(max(dims))
    spot[longest] = (spot[longest] + 1) % dims[longest]
    return drawn.at[tuple(spot)].set(high)


def shard_levels(rng, extent, shards, smallest, top_value):
    level = 1.0
    for position, shards_of in shards:
        heights = jax.random.uniform(jax.random.fold_in(jax.random.fold_in(rng, 6), position), (shards_of,), jnp.float32, smallest / len(shards), top_value / len(shards))
        level = level * jnp.repeat(jnp.exp(heights), extent[position] // shards_of).reshape((-1,) + (1,) * (len(extent) - 1 - position))
    return level


def shared_out(stream_key, own, number, rows, number_of, top, limit, lean):
    order = jax.random.permutation(stream_key, number_of)
    packed, usual = shares(number_of, rows * top, limit, lean, True), shares(number_of, rows * top, limit, lean, False)
    places = jnp.arange(number_of)

    def named(sizes, rotation):
        used = int((sizes > 0).sum())
        fixed = max(1, used // 4)
        shifted = fixed + (places - fixed + rotation * (used - fixed)) % max(1, number_of - fixed)
        return jnp.zeros((number_of,), jnp.int32).at[order[jnp.where(places < fixed, places, shifted)]].set(jnp.asarray(sizes, jnp.int32))

    sizes = jnp.where(number % 4 == 0, named(packed, number // 4), named(usual, number - number // 4 - 1))
    mixed = jax.random.permutation(jax.random.fold_in(own, 3), number_of)
    giver, taker = mixed[0:number_of // 2 * 2:2], mixed[1:number_of // 2 * 2:2]
    margin = jnp.minimum(sizes[giver] - 1, limit - sizes[taker]) // 2
    margin = jnp.where((giver == order[0]) | (taker == order[0]) | (sizes[taker] == 0), 0, jnp.maximum(margin, 0))
    shifted = jax.random.randint(jax.random.fold_in(own, 4), (number_of // 2,), 0, 1 << 20) % (margin + 1)
    sizes = sizes.at[giver].add(-shifted).at[taker].add(shifted)
    members = jnp.searchsorted(jnp.cumsum(sizes), jnp.arange(rows * top), side="right").astype(jnp.int32)
    listing = members.reshape(top, rows).T
    listing = listing[jax.random.permutation(jax.random.fold_in(own, 1), rows)]
    rotation = jax.random.randint(jax.random.fold_in(own, 2), (rows, 1), 0, top)
    return jnp.take_along_axis(listing, (jnp.arange(top)[None, :] + rotation) % top, axis=1)


def shares(number_of, total, most, skew, full):
    loads = [(1 << 20) // math.isqrt(rank ** skew) + 1 for rank in range(1, number_of + 1)]
    largest = most if full else min(most, max(-(-total // number_of), total * loads[0] // sum(loads)))
    least = 1 if total - largest >= number_of - 1 else 0
    given, rest = [largest] + [least] * (number_of - 1), total - largest - least * (number_of - 1)
    while rest > 0:
        movable = [i for i in range(1, number_of) if given[i] < largest] or [i for i in range(1, number_of) if given[i] < most]
        pool, remaining = sum([loads[i] for i in movable]), rest
        for i in movable:
            extra = min(most - given[i], max(1, remaining * loads[i] // pool), rest)
            given[i] = given[i] + extra
            rest = rest - extra
    return np.array(given)


def bell_draw(stream_key, dims, deviation, most, cuts=(), kind=jnp.bfloat16):
    array = deviation * jax.random.normal(stream_key, dims, jnp.float32)
    if cuts:
        array = array * shard_levels(stream_key, dims, cuts, -0.22, 0.18)
    return jnp.clip(array, -most, most).astype(kind)


def setup_inputs(seed: int = 0) -> dict:
    key_list = jax.random.split(jax.random.key(seed), 9)
    rhs = bell_draw(key_list[0], (TILES, NRHS, R), 1.0, 6.0, ((0, 128),), jnp.float32)
    jacobian = draw_jacobian(jax.random.fold_in(key_list[8], 71), 0)
    columns = draw_columns(jax.random.fold_in(key_list[8], 71), 0)
    send_tiles = with_ends(jax.random.randint(key_list[3], (SUBS * DOMS, 4, HB), 0, TPD), jax.random.fold_in(key_list[3], 1), 0, TPD - 1).astype(jnp.int32)
    smoother = draw_smoother(jax.random.fold_in(key_list[8], 71), 0)
    restriction = bell_draw(key_list[5], (TILES, R, R), (4 * R) ** -0.5, 0.25, ((0, 128),))
    coarse_inverse = draw_coarse_inverse(jax.random.fold_in(key_list[8], 71), 0)
    owner_keys = jax.random.split(jax.random.fold_in(key_list[7], 1), COARSE // CPD)
    owner_turns = jax.random.permutation(jax.random.fold_in(key_list[7], 3), COARSE // CPD)
    owner = jax.vmap(lambda own, number: shared_out(jax.random.fold_in(key_list[7], 2), own, number, CPD, DOMS, 1, CAP, 2))(owner_keys, owner_turns).reshape((COARSE, 1))
    return {"rhs": rhs, "jacobian": jacobian, "columns": columns, "send_tiles": send_tiles, "smoother": smoother, "restriction": restriction, "coarse_inverse": coarse_inverse, "owner": owner}


OMEGA = 0.8


def reference(rhs, jacobian, columns, send_tiles, smoother, restriction, coarse_inverse, owner):
    domains = SUBS * DOMS
    mats = jacobian.reshape(domains, TPD, K, R, R)
    cols = columns.reshape(domains, TPD, K)
    sends = send_tiles.reshape(SUBS, DOMS, 4, HB)
    smooth = smoother.reshape(domains, TPD, R, R)
    restrict = restriction.reshape(domains, TPD, R, R)
    target = rhs.reshape(domains, TPD, NRHS, R)
    pick = jax.vmap(jax.vmap(lambda table, index: table[index]))

    def extend(vector_bf):
        whole = vector_bf.reshape(SUBS, DOMS, TPD, NRHS, R)
        packs = [pick(whole, sends[:, :, j]) for j in range(4)]
        zero_dev = jnp.zeros_like(packs[0][:, :1])
        zero_grp = jnp.zeros_like(packs[2][:1])
        from_left = jnp.concatenate([zero_dev, packs[0][:, :-1]], axis=1)
        from_right = jnp.concatenate([packs[1][:, 1:], zero_dev], axis=1)
        from_low = jnp.concatenate([zero_grp, packs[2][:-1]], axis=0)
        from_high = jnp.concatenate([packs[3][1:], zero_grp], axis=0)
        joined = jnp.concatenate([whole, from_left, from_right, from_low, from_high], axis=2)
        return joined.reshape(domains, TPD + 4 * HB, NRHS, R)

    def operate(state):
        extended = extend(state.astype(jnp.bfloat16))

        def one_domain(pieces):
            tiles_here, cols_here, ext_here = pieces
            gathered = ext_here[cols_here]
            return jnp.einsum('tkij,tkrj->tri', tiles_here.astype(jnp.float32), gathered.astype(jnp.float32))

        return lax.map(one_domain, (mats, cols, extended))

    def tiles_apply(matrices, vectors, form):
        return lax.map(lambda pieces: jnp.einsum(form, pieces[0].astype(jnp.float32), pieces[1].astype(jnp.float32)), (matrices, vectors))

    def jacobi(vectors):
        return tiles_apply(smooth, vectors.astype(jnp.bfloat16), 'tij,trj->tri')

    state = OMEGA * jacobi(target)
    for sweep in range(SWEEPS - 1):
        state = state + OMEGA * jacobi(target - operate(state))
    residual = target - operate(state)
    restricted = tiles_apply(restrict, residual.astype(jnp.bfloat16), 'tij,trj->tri')
    coarse = restricted.reshape(SUBS, DOMS, CPD, AGG, NRHS, R).sum(axis=(0, 3))
    owners = owner[:, 0].reshape(DOMS, CPD)
    order = jnp.arange(CPD, dtype=jnp.int32)
    earlier = (owners[:, :, None] == owners[:, None, :]) & (order[None, None, :] < order[None, :, None])
    slot = jnp.sum(earlier.astype(jnp.int32), axis=2)
    source = jnp.broadcast_to(jnp.arange(DOMS, dtype=jnp.int32)[:, None], (DOMS, CPD))
    picked = coarse_inverse[owners, source, slot]
    coarse_fix = jnp.einsum('dcab,dcrb->dcra', picked.astype(jnp.float32), coarse.astype(jnp.bfloat16).astype(jnp.float32)).astype(jnp.bfloat16)
    fine_fix = jnp.repeat(coarse_fix, AGG, axis=1)
    fine_fix = jnp.broadcast_to(fine_fix[None], (SUBS, DOMS, TPD, NRHS, R)).reshape(domains, TPD, NRHS, R)
    state = state + tiles_apply(restrict, fine_fix, 'tji,trj->tri')
    for sweep in range(SWEEPS):
        state = state + OMEGA * jacobi(target - operate(state))
    return state.reshape(TILES, NRHS, R)
```

```python
import functools

import jax
import jax.numpy as jnp
from jax import lax
from jax.experimental import pallas as pl
from jax.experimental.pallas import tpu as pltpu
from jax.sharding import PartitionSpec as P

AGG = 2
SWEEPS = 3


OMEGA = 0.8
BLOCK = 8


def shifted(value, axis, by):
    length = lax.axis_size(axis)
    pairs = [(i, i + by) for i in range(length) if 0 <= i + by < length]
    return lax.ppermute(value, axis, pairs)


def dev_rim(pack, offset):
    return shifted(pack, "dev", offset)


def grp_rim(pack, offset):
    return shifted(pack, "grp", offset)


def _nt(a, b):
    return lax.dot_general(a, b, (((1,), (1,)), ((), ())), preferred_element_type=jnp.float32)


def _sweep_kernel(cols_ref, x_ref, rhs_ref, jac_ref, sm_ref, own_ref, h0_ref, h1_ref, h2_ref, h3_ref,
                  out_ref, outbf_ref, *, stored, rim, tile_count, first):
    base = pl.program_id(0) * BLOCK
    halos = (h0_ref, h1_ref, h2_ref, h3_ref)
    for i in range(BLOCK):
        n = base + i
        acc = None
        for k in range(stored):
            col = cols_ref[n * stored + k]
            if k < 3:
                tile = own_ref[jnp.clip(col, 0, tile_count - 1)]
            else:
                j = k - 3
                tile = halos[j][jnp.clip(col - tile_count - j * rim, 0, rim - 1)]
            part = _nt(tile, jac_ref[i, k])
            acc = part if acc is None else acc + part
        v = (rhs_ref[i] - acc).astype(jnp.bfloat16)
        new = x_ref[i] + OMEGA * _nt(v, sm_ref[i])
        out_ref[i] = new
        outbf_ref[i] = new.astype(jnp.bfloat16)


def sweep(cols_flat, x, x_bf, rhs, jacobian, smoother, halos):
    tile_count, vectors_count, tile_rows = x.shape
    stored = jacobian.shape[1]
    rim = halos[0].shape[0]
    blocked = lambda i, c: (i, 0, 0)
    whole = lambda i, c: (0, 0, 0)
    kernel = functools.partial(_sweep_kernel, stored=stored, rim=rim, tile_count=tile_count, first=False)
    tile_spec = pl.BlockSpec((BLOCK, vectors_count, tile_rows), blocked)
    grid_spec = pltpu.PrefetchScalarGridSpec(
        num_scalar_prefetch=1,
        grid=(tile_count // BLOCK,),
        in_specs=[
            tile_spec,
            tile_spec,
            pl.BlockSpec((BLOCK, stored, tile_rows, tile_rows), lambda i, c: (i, 0, 0, 0)),
            pl.BlockSpec((BLOCK, tile_rows, tile_rows), blocked),
            pl.BlockSpec((tile_count, vectors_count, tile_rows), whole),
        ]
        + [pl.BlockSpec((rim, vectors_count, tile_rows), whole) for _ in range(4)],
        out_specs=[tile_spec, tile_spec],
    )
    return pl.pallas_call(
        kernel,
        grid_spec=grid_spec,
        out_shape=[
            jax.ShapeDtypeStruct(x.shape, jnp.float32),
            jax.ShapeDtypeStruct(x.shape, jnp.bfloat16),
        ],
        compiler_params=pltpu.CompilerParams(dimension_semantics=("arbitrary",)),
    )(cols_flat, x, rhs, jacobian, smoother, x_bf, *halos)


def shards(rhs, jacobian, columns, send_tiles, smoother, restriction, coarse_inverse, owner):
    tile_count = rhs.shape[0]
    vectors_count = rhs.shape[1]
    tile_rows = rhs.shape[2]
    domains_dev = lax.axis_size("dev")
    capacity = coarse_inverse.shape[2]
    blocks = tile_count // AGG
    listed = send_tiles[0]
    rim_count = listed.shape[1]
    cols_flat = columns.reshape(-1)
    listed_flat = jnp.clip(listed.reshape(-1), 0, tile_count - 1)

    def exchange(state_bf):
        packs = jnp.take(state_bf, listed_flat, axis=0)
        packs = packs.reshape(4, rim_count, vectors_count, tile_rows)
        from_left = dev_rim(packs[0], 1)
        from_right = dev_rim(packs[1], -1)
        from_low = grp_rim(packs[2], 1)
        from_high = grp_rim(packs[3], -1)
        return (from_left, from_right, from_low, from_high)

    def smooth(state, state_bf):
        return sweep(cols_flat, state, state_bf, rhs, jacobian, smoother, exchange(state_bf))

    def jacobi(vectors):
        return jnp.einsum(
            "tij,trj->tri",
            smoother,
            vectors.astype(jnp.bfloat16),
            preferred_element_type=jnp.float32,
        )

    def operate(state_bf, halos):
        extended = jnp.concatenate([state_bf, *halos], axis=0)
        gathered = jnp.take(extended, columns, axis=0)
        return jnp.einsum("tkij,tkrj->tri", jacobian, gathered, preferred_element_type=jnp.float32)

    position = lax.axis_index("dev")
    mine = lax.dynamic_slice_in_dim(owner[:, 0], position * blocks, blocks)
    order = jnp.arange(blocks, dtype=jnp.int32)
    earlier = (mine[:, None] == mine[None, :]) & (order[None, :] < order[:, None])
    slot = jnp.sum(earlier.astype(jnp.int32), axis=1)
    state = OMEGA * jacobi(rhs)
    state_bf = state.astype(jnp.bfloat16)
    for sweep_index in range(SWEEPS - 1):
        state, state_bf = smooth(state, state_bf)
    residual = rhs - operate(state_bf, exchange(state_bf))
    restricted = jnp.einsum(
        "tij,trj->tri",
        restriction,
        residual.astype(jnp.bfloat16),
        preferred_element_type=jnp.float32,
    )
    partial_sum = restricted.reshape(blocks, AGG, vectors_count, tile_rows).sum(axis=1)
    coarse = lax.psum(partial_sum.astype(jnp.bfloat16), "grp")
    outgoing = jnp.zeros((domains_dev, capacity, vectors_count, tile_rows), jnp.bfloat16)
    outgoing = outgoing.at[mine, slot].set(coarse)
    arrived = lax.all_to_all(outgoing, "dev", split_axis=0, concat_axis=0, tiled=True)
    solved = jnp.einsum(
        "sjab,sjrb->sjra", coarse_inverse[0], arrived, preferred_element_type=jnp.float32
    ).astype(jnp.bfloat16)
    returned = lax.all_to_all(solved, "dev", split_axis=0, concat_axis=0, tiled=True)
    coarse_fix = returned[mine, slot]
    fine_fix = jnp.repeat(coarse_fix, AGG, axis=0)
    state = state + jnp.einsum(
        "tji,trj->tri", restriction, fine_fix, preferred_element_type=jnp.float32
    )
    state_bf = state.astype(jnp.bfloat16)
    for sweep_index in range(SWEEPS):
        state, state_bf = smooth(state, state_bf)
    return state


def solution(mesh):
    in_specs = (
        P(("grp", "dev"), None, None),
        P(("grp", "dev"), None, None, None),
        P(("grp", "dev"), None),
        P(("grp", "dev"), None, None),
        P(("grp", "dev"), None, None),
        P(("grp", "dev"), None, None),
        P("dev", None, None, None, None),
        P(),
    )
    out_specs = P(("grp", "dev"), None, None)
    return jax.shard_map(shards, mesh=mesh, in_specs=in_specs, out_specs=out_specs, check_vma=False)
```

```python
import jax
import jax.numpy as jnp
from jax import lax
from jax.sharding import PartitionSpec as P

AGG = 2
SWEEPS = 3


OMEGA = 0.8


def shifted(value, axis, by):
    length = lax.axis_size(axis)
    pairs = [(i, i + by) for i in range(length) if 0 <= i + by < length]
    return lax.ppermute(value, axis, pairs)


def dev_rim(pack, offset):
    return shifted(pack, "dev", offset)


def grp_rim(pack, offset):
    return shifted(pack, "grp", offset)


def grp_sum(value):
    length = lax.axis_size("grp")
    total = value.astype(jnp.float32)
    for by in range(1, length):
        pairs = [(i, (i + by) % length) for i in range(length)]
        total = total + lax.ppermute(value, "grp", pairs).astype(jnp.float32)
    return total.astype(jnp.bfloat16)


def shards(rhs, jacobian, columns, send_tiles, smoother, restriction, coarse_inverse, owner):
    tile_count = rhs.shape[0]
    vectors_count = rhs.shape[1]
    tile_rows = rhs.shape[2]
    stored = columns.shape[1]
    domains_dev = lax.axis_size("dev")
    capacity = coarse_inverse.shape[2]
    blocks = tile_count // AGG
    listed = send_tiles[0]
    rim_count = listed.shape[1]
    ext_count = tile_count + 4 * rim_count
    flat_width = vectors_count * tile_rows
    ext_range = jnp.arange(ext_count, dtype=jnp.int32)
    column_select = (columns.reshape(-1)[:, None] == ext_range[None, :]).astype(jnp.bfloat16)
    own_range = jnp.arange(tile_count, dtype=jnp.int32)
    rim_select = (listed.reshape(-1)[:, None] == own_range[None, :]).astype(jnp.bfloat16)

    def operate(state):
        state_bf = state.astype(jnp.bfloat16)
        state_flat = state_bf.reshape(tile_count, flat_width)
        packs = jnp.dot(rim_select, state_flat, preferred_element_type=jnp.float32).astype(
            jnp.bfloat16
        )
        packs = packs.reshape(4, rim_count, vectors_count, tile_rows)
        from_left = dev_rim(packs[0], 1)
        from_right = dev_rim(packs[1], -1)
        from_low = grp_rim(packs[2], 1)
        from_high = grp_rim(packs[3], -1)
        extended = jnp.concatenate([state_bf, from_left, from_right, from_low, from_high], axis=0)
        gathered = jnp.dot(
            column_select,
            extended.reshape(ext_count, flat_width),
            preferred_element_type=jnp.float32,
        ).astype(jnp.bfloat16)
        gathered = gathered.reshape(tile_count, stored, vectors_count, tile_rows)
        return jnp.einsum("tkij,tkrj->tri", jacobian, gathered, preferred_element_type=jnp.float32)

    def jacobi(vectors):
        return jnp.einsum(
            "tij,trj->tri",
            smoother,
            vectors.astype(jnp.bfloat16),
            preferred_element_type=jnp.float32,
        )

    position = lax.axis_index("dev")
    mine = lax.dynamic_slice_in_dim(owner[:, 0], position * blocks, blocks)
    order = jnp.arange(blocks, dtype=jnp.int32)
    earlier = (mine[:, None] == mine[None, :]) & (order[None, :] < order[:, None])
    slot = jnp.sum(earlier.astype(jnp.int32), axis=1)
    state = OMEGA * jacobi(rhs)
    for sweep in range(SWEEPS - 1):
        state = state + OMEGA * jacobi(rhs - operate(state))
    residual = rhs - operate(state)
    restricted = jnp.einsum(
        "tij,trj->tri",
        restriction,
        residual.astype(jnp.bfloat16),
        preferred_element_type=jnp.float32,
    )
    partial_sum = restricted.reshape(blocks, AGG, vectors_count, tile_rows).sum(axis=1)
    coarse = grp_sum(partial_sum.astype(jnp.bfloat16))
    outgoing = jnp.zeros((domains_dev, capacity, vectors_count, tile_rows), jnp.bfloat16)
    outgoing = outgoing.at[mine, slot].set(coarse)
    arrived = lax.all_to_all(outgoing, "dev", split_axis=0, concat_axis=0, tiled=True)
    solved = jnp.einsum(
        "sjab,sjrb->sjra", coarse_inverse[0], arrived, preferred_element_type=jnp.float32
    ).astype(jnp.bfloat16)
    returned = lax.all_to_all(solved, "dev", split_axis=0, concat_axis=0, tiled=True)
    coarse_fix = returned[mine, slot]
    fine_fix = jnp.repeat(coarse_fix, AGG, axis=0)
    state = state + jnp.einsum(
        "tji,trj->tri", restriction, fine_fix, preferred_element_type=jnp.float32
    )
    for sweep in range(SWEEPS):
        state = state + OMEGA * jacobi(rhs - operate(state))
    return state


def solution(mesh):
    in_specs = (
        P(("grp", "dev"), None, None),
        P(("grp", "dev"), None, None, None),
        P(("grp", "dev"), None),
        P(("grp", "dev"), None, None),
        P(("grp", "dev"), None, None),
        P(("grp", "dev"), None, None),
        P("dev", None, None, None, None),
        P(),
    )
    out_specs = P(("grp", "dev"), None, None)
    return jax.shard_map(shards, mesh=mesh, in_specs=in_specs, out_specs=out_specs, check_vma=False)
```

```python
import jax
import jax.numpy as jnp
from jax import lax
from jax.sharding import PartitionSpec as P

AGG = 2
SWEEPS = 3


OMEGA = 0.8


def shifted(value, axis, by):
    length = lax.axis_size(axis)
    pairs = [(i, i + by) for i in range(length) if 0 <= i + by < length]
    return lax.ppermute(value, axis, pairs)


def dev_rim(pack, offset):
    return shifted(pack, "dev", offset)


def grp_rim(pack, offset):
    return shifted(pack, "grp", offset)


def grp_sum(value):
    length = lax.axis_size("grp")
    total = value.astype(jnp.float32)
    for by in range(1, length):
        pairs = [(i, (i + by) % length) for i in range(length)]
        total = total + lax.ppermute(value, "grp", pairs).astype(jnp.float32)
    return total.astype(jnp.bfloat16)


def shards(rhs, jacobian, columns, send_tiles, smoother, restriction, coarse_inverse, owner):
    tile_count = rhs.shape[0]
    vectors_count = rhs.shape[1]
    tile_rows = rhs.shape[2]
    stored = columns.shape[1]
    blocks = tile_count // AGG
    listed = send_tiles[0]
    rim_count = listed.shape[1]
    ext_count = tile_count + 4 * rim_count
    flat_width = vectors_count * tile_rows
    ext_range = jnp.arange(ext_count, dtype=jnp.int32)
    column_select = (columns.reshape(-1)[:, None] == ext_range[None, :]).astype(jnp.bfloat16)
    own_range = jnp.arange(tile_count, dtype=jnp.int32)
    rim_select = (listed.reshape(-1)[:, None] == own_range[None, :]).astype(jnp.bfloat16)

    def operate(state):
        state_bf = state.astype(jnp.bfloat16)
        state_flat = state_bf.reshape(tile_count, flat_width)
        packs = jnp.dot(rim_select, state_flat, preferred_element_type=jnp.float32).astype(
            jnp.bfloat16
        )
        packs = packs.reshape(4, rim_count, vectors_count, tile_rows)
        from_left = dev_rim(packs[0], 1)
        from_right = dev_rim(packs[1], -1)
        from_low = grp_rim(packs[2], 1)
        from_high = grp_rim(packs[3], -1)
        extended = jnp.concatenate([state_bf, from_left, from_right, from_low, from_high], axis=0)
        gathered = jnp.dot(
            column_select,
            extended.reshape(ext_count, flat_width),
            preferred_element_type=jnp.float32,
        ).astype(jnp.bfloat16)
        gathered = gathered.reshape(tile_count, stored, vectors_count, tile_rows)
        return jnp.einsum("tkij,tkrj->tri", jacobian, gathered, preferred_element_type=jnp.float32)

    def jacobi(vectors):
        return jnp.einsum(
            "tij,trj->tri",
            smoother,
            vectors.astype(jnp.bfloat16),
            preferred_element_type=jnp.float32,
        )

    position = lax.axis_index("dev")
    mine = lax.dynamic_slice_in_dim(owner[:, 0], position * blocks, blocks)
    order = jnp.arange(blocks, dtype=jnp.int32)
    earlier = (mine[:, None] == mine[None, :]) & (order[None, :] < order[:, None])
    slot = jnp.sum(earlier.astype(jnp.int32), axis=1)
    fetched = lax.all_to_all(coarse_inverse[0], "dev", split_axis=0, concat_axis=0, tiled=True)
    picked = fetched[mine, slot]
    state = OMEGA * jacobi(rhs)
    for sweep in range(SWEEPS - 1):
        state = state + OMEGA * jacobi(rhs - operate(state))
    residual = rhs - operate(state)
    restricted = jnp.einsum(
        "tij,trj->tri",
        restriction,
        residual.astype(jnp.bfloat16),
        preferred_element_type=jnp.float32,
    )
    partial_sum = restricted.reshape(blocks, AGG, vectors_count, tile_rows).sum(axis=1)
    coarse = grp_sum(partial_sum.astype(jnp.bfloat16))
    solved = jnp.einsum("cab,crb->cra", picked, coarse, preferred_element_type=jnp.float32)
    coarse_fix = solved.astype(jnp.bfloat16)
    fine_fix = jnp.repeat(coarse_fix, AGG, axis=0)
    state = state + jnp.einsum(
        "tji,trj->tri", restriction, fine_fix, preferred_element_type=jnp.float32
    )
    for sweep in range(SWEEPS):
        state = state + OMEGA * jacobi(rhs - operate(state))
    return state


def solution(mesh):
    in_specs = (
        P(("grp", "dev"), None, None),
        P(("grp", "dev"), None, None, None),
        P(("grp", "dev"), None),
        P(("grp", "dev"), None, None),
        P(("grp", "dev"), None, None),
        P(("grp", "dev"), None, None),
        P("dev", None, None, None, None),
        P(),
    )
    out_specs = P(("grp", "dev"), None, None)
    return jax.shard_map(shards, mesh=mesh, in_specs=in_specs, out_specs=out_specs, check_vma=False)
```

```python
import jax
import jax.numpy as jnp
from jax import lax
from jax.sharding import PartitionSpec as P

AGG = 2
SWEEPS = 3


OMEGA = 0.8


def shifted(value, axis, by):
    length = lax.axis_size(axis)
    pairs = [(i, i + by) for i in range(length) if 0 <= i + by < length]
    return lax.ppermute(value, axis, pairs)


def dev_rim(pack, offset):
    return shifted(pack, "dev", offset)


def grp_rim(pack, offset):
    return shifted(pack, "grp", offset)


def grp_sum(value):
    length = lax.axis_size("grp")
    total = value.astype(jnp.float32)
    for by in range(1, length):
        pairs = [(i, (i + by) % length) for i in range(length)]
        total = total + lax.ppermute(value, "grp", pairs).astype(jnp.float32)
    return total.astype(jnp.bfloat16)


def shards(rhs, jacobian, columns, send_tiles, smoother, restriction, coarse_inverse, owner):
    tile_count = rhs.shape[0]
    vectors_count = rhs.shape[1]
    tile_rows = rhs.shape[2]
    stored = columns.shape[1]
    blocks = tile_count // AGG
    listed = send_tiles[0]
    rim_count = listed.shape[1]
    flat_width = vectors_count * tile_rows
    local_count = 3
    own_range = jnp.arange(tile_count, dtype=jnp.int32)
    rim_range = tile_count + jnp.arange(4 * rim_count, dtype=jnp.int32)
    local_select = (columns[:, :local_count].reshape(-1)[:, None] == own_range[None, :]).astype(jnp.bfloat16)
    halo_select = (columns[:, local_count:].reshape(-1)[:, None] == rim_range[None, :]).astype(jnp.bfloat16)
    rim_select = (listed.reshape(-1)[:, None] == own_range[None, :]).astype(jnp.bfloat16)
    local_jacobian = jacobian[:, :local_count]
    halo_jacobian = jacobian[:, local_count:]

    def operate(state):
        state_bf = state.astype(jnp.bfloat16)
        state_flat = state_bf.reshape(tile_count, flat_width)
        packs = jnp.dot(rim_select, state_flat, preferred_element_type=jnp.float32).astype(
            jnp.bfloat16
        )
        packs = packs.reshape(4, rim_count, vectors_count, tile_rows)
        from_left = dev_rim(packs[0], 1)
        from_right = dev_rim(packs[1], -1)
        from_low = grp_rim(packs[2], 1)
        from_high = grp_rim(packs[3], -1)
        near = jnp.dot(local_select, state_flat, preferred_element_type=jnp.float32).astype(jnp.bfloat16)
        near = near.reshape(tile_count, local_count, vectors_count, tile_rows)
        inner = jnp.einsum("tkij,tkrj->tri", local_jacobian, near, preferred_element_type=jnp.float32)
        inner = lax.optimization_barrier(inner)
        rims = jnp.concatenate([from_left, from_right, from_low, from_high], axis=0)
        far = jnp.dot(
            halo_select,
            rims.reshape(4 * rim_count, flat_width),
            preferred_element_type=jnp.float32,
        ).astype(jnp.bfloat16)
        far = far.reshape(tile_count, stored - local_count, vectors_count, tile_rows)
        return inner + jnp.einsum("tkij,tkrj->tri", halo_jacobian, far, preferred_element_type=jnp.float32)

    def jacobi(vectors):
        return jnp.einsum(
            "tij,trj->tri",
            smoother,
            vectors.astype(jnp.bfloat16),
            preferred_element_type=jnp.float32,
        )

    position = lax.axis_index("dev")
    mine = lax.dynamic_slice_in_dim(owner[:, 0], position * blocks, blocks)
    order = jnp.arange(blocks, dtype=jnp.int32)
    earlier = (mine[:, None] == mine[None, :]) & (order[None, :] < order[:, None])
    slot = jnp.sum(earlier.astype(jnp.int32), axis=1)
    fetched = lax.all_to_all(coarse_inverse[0], "dev", split_axis=0, concat_axis=0, tiled=True)
    picked = fetched[mine, slot]
    state = OMEGA * jacobi(rhs)
    for sweep in range(SWEEPS - 1):
        state = state + OMEGA * jacobi(rhs - operate(state))
    residual = rhs - operate(state)
    restricted = jnp.einsum(
        "tij,trj->tri",
        restriction,
        residual.astype(jnp.bfloat16),
        preferred_element_type=jnp.float32,
    )
    partial_sum = restricted.reshape(blocks, AGG, vectors_count, tile_rows).sum(axis=1)
    coarse = grp_sum(partial_sum.astype(jnp.bfloat16))
    solved = jnp.einsum("cab,crb->cra", picked, coarse, preferred_element_type=jnp.float32)
    coarse_fix = solved.astype(jnp.bfloat16)
    fine_fix = jnp.repeat(coarse_fix, AGG, axis=0)
    state = state + jnp.einsum(
        "tji,trj->tri", restriction, fine_fix, preferred_element_type=jnp.float32
    )
    for sweep in range(SWEEPS):
        state = state + OMEGA * jacobi(rhs - operate(state))
    return state


def solution(mesh):
    in_specs = (
        P(("grp", "dev"), None, None),
        P(("grp", "dev"), None, None, None),
        P(("grp", "dev"), None),
        P(("grp", "dev"), None, None),
        P(("grp", "dev"), None, None),
        P(("grp", "dev"), None, None),
        P("dev", None, None, None, None),
        P(),
    )
    out_specs = P(("grp", "dev"), None, None)
    return jax.shard_map(shards, mesh=mesh, in_specs=in_specs, out_specs=out_specs, check_vma=False)
```

```python
import functools

import jax
import jax.numpy as jnp
from jax import lax
from jax.experimental import pallas as pl
from jax.experimental.pallas import tpu as pltpu
from jax.sharding import PartitionSpec as P

AGG = 2
SWEEPS = 3


OMEGA = 0.8
BLOCK = 8


def _rim_kernel(cols_ref, x_ref, rhs_ref, inner_ref, jt_ref, st_ref, h0_ref, h1_ref, h2_ref, h3_ref,
                out_ref, outbf_ref, *, tile_count, rim):
    base = pl.program_id(0) * BLOCK
    halos = (h0_ref, h1_ref, h2_ref, h3_ref)
    for i in range(BLOCK):
        n = base + i
        tiles = []
        for j in range(4):
            col = cols_ref[n * 4 + j] - tile_count - j * rim
            tiles.append(halos[j][jnp.clip(col, 0, rim - 1)])
        gathered = jnp.concatenate(tiles, axis=1)
        acc = inner_ref[i] + jnp.dot(gathered, jt_ref[i], preferred_element_type=jnp.float32)
        v = (rhs_ref[i] - acc).astype(jnp.bfloat16)
        new = x_ref[i] + OMEGA * jnp.dot(v, st_ref[i], preferred_element_type=jnp.float32)
        out_ref[i] = new
        outbf_ref[i] = new.astype(jnp.bfloat16)


def rim_sweep(cols_flat, x, rhs, inner, jt, st, halos):
    tile_count, vectors_count, tile_rows = x.shape
    rim = halos[0].shape[0]
    blocked = lambda i, c: (i, 0, 0)
    whole = lambda i, c: (0, 0, 0)
    tile_spec = pl.BlockSpec((BLOCK, vectors_count, tile_rows), blocked)
    grid_spec = pltpu.PrefetchScalarGridSpec(
        num_scalar_prefetch=1,
        grid=(tile_count // BLOCK,),
        in_specs=[
            tile_spec,
            tile_spec,
            tile_spec,
            pl.BlockSpec((BLOCK, jt.shape[1], tile_rows), blocked),
            pl.BlockSpec((BLOCK, tile_rows, tile_rows), blocked),
        ]
        + [pl.BlockSpec((rim, vectors_count, tile_rows), whole) for _ in range(4)],
        out_specs=[tile_spec, tile_spec],
    )
    kernel = functools.partial(_rim_kernel, tile_count=tile_count, rim=rim)
    return pl.pallas_call(
        kernel,
        grid_spec=grid_spec,
        out_shape=[
            jax.ShapeDtypeStruct(x.shape, jnp.float32),
            jax.ShapeDtypeStruct(x.shape, jnp.bfloat16),
        ],
    )(cols_flat, x, rhs, inner, jt, st, *halos)


def shifted(value, axis, by):
    length = lax.axis_size(axis)
    pairs = [(i, i + by) for i in range(length) if 0 <= i + by < length]
    return lax.ppermute(value, axis, pairs)


def dev_rim(pack, offset):
    return shifted(pack, "dev", offset)


def grp_rim(pack, offset):
    return shifted(pack, "grp", offset)


def grp_sum(value):
    length = lax.axis_size("grp")
    total = value.astype(jnp.float32)
    for by in range(1, length):
        pairs = [(i, (i + by) % length) for i in range(length)]
        total = total + lax.ppermute(value, "grp", pairs).astype(jnp.float32)
    return total.astype(jnp.bfloat16)


def shards(rhs, jacobian, columns, send_tiles, smoother, restriction, coarse_inverse, owner):
    tile_count = rhs.shape[0]
    vectors_count = rhs.shape[1]
    tile_rows = rhs.shape[2]
    stored = columns.shape[1]
    blocks = tile_count // AGG
    listed = send_tiles[0]
    rim_count = listed.shape[1]
    flat_width = vectors_count * tile_rows
    local_count = 3
    own_range = jnp.arange(tile_count, dtype=jnp.int32)
    rim_range = tile_count + jnp.arange(4 * rim_count, dtype=jnp.int32)
    local_select = (columns[:, :local_count].reshape(-1)[:, None] == own_range[None, :]).astype(jnp.bfloat16)
    halo_select = (columns[:, local_count:].reshape(-1)[:, None] == rim_range[None, :]).astype(jnp.bfloat16)
    rim_select = (listed.reshape(-1)[:, None] == own_range[None, :]).astype(jnp.bfloat16)
    local_jacobian = jacobian[:, :local_count]
    halo_jacobian = jacobian[:, local_count:]

    def operate(state):
        state_bf = state.astype(jnp.bfloat16)
        state_flat = state_bf.reshape(tile_count, flat_width)
        packs = jnp.dot(rim_select, state_flat, preferred_element_type=jnp.float32).astype(
            jnp.bfloat16
        )
        packs = packs.reshape(4, rim_count, vectors_count, tile_rows)
        from_left = dev_rim(packs[0], 1)
        from_right = dev_rim(packs[1], -1)
        from_low = grp_rim(packs[2], 1)
        from_high = grp_rim(packs[3], -1)
        near = jnp.dot(local_select, state_flat, preferred_element_type=jnp.float32).astype(jnp.bfloat16)
        near = near.reshape(tile_count, local_count, vectors_count, tile_rows)
        inner = jnp.einsum("tkij,tkrj->tri", local_jacobian, near, preferred_element_type=jnp.float32)
        inner = lax.optimization_barrier(inner)
        rims = jnp.concatenate([from_left, from_right, from_low, from_high], axis=0)
        far = jnp.dot(
            halo_select,
            rims.reshape(4 * rim_count, flat_width),
            preferred_element_type=jnp.float32,
        ).astype(jnp.bfloat16)
        far = far.reshape(tile_count, stored - local_count, vectors_count, tile_rows)
        return inner + jnp.einsum("tkij,tkrj->tri", halo_jacobian, far, preferred_element_type=jnp.float32)

    halo_cols = columns[:, local_count:].reshape(-1)
    halo_jt = jnp.swapaxes(halo_jacobian, 2, 3).reshape(tile_count, (stored - local_count) * tile_rows, tile_rows)
    smoother_t = jnp.swapaxes(smoother, 1, 2)

    def smooth(state, state_bf):
        state_flat = state_bf.reshape(tile_count, flat_width)
        packs = jnp.dot(rim_select, state_flat, preferred_element_type=jnp.float32).astype(
            jnp.bfloat16
        )
        packs = packs.reshape(4, rim_count, vectors_count, tile_rows)
        halos = (dev_rim(packs[0], 1), dev_rim(packs[1], -1), grp_rim(packs[2], 1), grp_rim(packs[3], -1))
        near = jnp.dot(local_select, state_flat, preferred_element_type=jnp.float32).astype(jnp.bfloat16)
        near = near.reshape(tile_count, local_count, vectors_count, tile_rows)
        inner = jnp.einsum("tkij,tkrj->tri", local_jacobian, near, preferred_element_type=jnp.float32)
        inner = lax.optimization_barrier(inner)
        return rim_sweep(halo_cols, state, rhs, inner, halo_jt, smoother_t, halos)

    def jacobi(vectors):
        return jnp.einsum(
            "tij,trj->tri",
            smoother,
            vectors.astype(jnp.bfloat16),
            preferred_element_type=jnp.float32,
        )

    position = lax.axis_index("dev")
    mine = lax.dynamic_slice_in_dim(owner[:, 0], position * blocks, blocks)
    order = jnp.arange(blocks, dtype=jnp.int32)
    earlier = (mine[:, None] == mine[None, :]) & (order[None, :] < order[:, None])
    slot = jnp.sum(earlier.astype(jnp.int32), axis=1)
    fetched = lax.all_to_all(coarse_inverse[0], "dev", split_axis=0, concat_axis=0, tiled=True)
    picked = fetched[mine, slot]
    state = OMEGA * jacobi(rhs)
    state_bf = state.astype(jnp.bfloat16)
    for sweep in range(SWEEPS - 1):
        state, state_bf = smooth(state, state_bf)
    residual = rhs - operate(state)
    restricted = jnp.einsum(
        "tij,trj->tri",
        restriction,
        residual.astype(jnp.bfloat16),
        preferred_element_type=jnp.float32,
    )
    partial_sum = restricted.reshape(blocks, AGG, vectors_count, tile_rows).sum(axis=1)
    coarse = grp_sum(partial_sum.astype(jnp.bfloat16))
    solved = jnp.einsum("cab,crb->cra", picked, coarse, preferred_element_type=jnp.float32)
    coarse_fix = solved.astype(jnp.bfloat16)
    fine_fix = jnp.repeat(coarse_fix, AGG, axis=0)
    state = state + jnp.einsum(
        "tji,trj->tri", restriction, fine_fix, preferred_element_type=jnp.float32
    )
    state_bf = state.astype(jnp.bfloat16)
    for sweep in range(SWEEPS):
        state, state_bf = smooth(state, state_bf)
    return state


def solution(mesh):
    in_specs = (
        P(("grp", "dev"), None, None),
        P(("grp", "dev"), None, None, None),
        P(("grp", "dev"), None),
        P(("grp", "dev"), None, None),
        P(("grp", "dev"), None, None),
        P(("grp", "dev"), None, None),
        P("dev", None, None, None, None),
        P(),
    )
    out_specs = P(("grp", "dev"), None, None)
    return jax.shard_map(shards, mesh=mesh, in_specs=in_specs, out_specs=out_specs, check_vma=False)
```

```python
import jax
import jax.numpy as jnp
from jax import lax
from jax.sharding import PartitionSpec as P

AGG = 2
SWEEPS = 3


OMEGA = 0.8


def shifted(value, axis, by):
    length = lax.axis_size(axis)
    pairs = [(i, i + by) for i in range(length) if 0 <= i + by < length]
    return lax.ppermute(value, axis, pairs)


def dev_rim(pack, offset):
    return shifted(pack, "dev", offset)


def grp_rim(pack, offset):
    return shifted(pack, "grp", offset)


def shards(rhs, jacobian, columns, send_tiles, smoother, restriction, coarse_inverse, owner):
    tile_count = rhs.shape[0]
    vectors_count = rhs.shape[1]
    tile_rows = rhs.shape[2]
    stored = columns.shape[1]
    blocks = tile_count // AGG
    listed = send_tiles[0]
    rim_count = listed.shape[1]
    ext_count = tile_count + 4 * rim_count
    flat_width = vectors_count * tile_rows
    ext_range = jnp.arange(ext_count, dtype=jnp.int32)
    column_select = (columns.reshape(-1)[:, None] == ext_range[None, :]).astype(jnp.bfloat16)
    own_range = jnp.arange(tile_count, dtype=jnp.int32)
    rim_select = (listed.reshape(-1)[:, None] == own_range[None, :]).astype(jnp.bfloat16)

    def operate(state):
        state_bf = state.astype(jnp.bfloat16)
        state_flat = state_bf.reshape(tile_count, flat_width)
        packs = jnp.dot(rim_select, state_flat, preferred_element_type=jnp.float32).astype(
            jnp.bfloat16
        )
        packs = packs.reshape(4, rim_count, vectors_count, tile_rows)
        from_left = dev_rim(packs[0], 1)
        from_right = dev_rim(packs[1], -1)
        from_low = grp_rim(packs[2], 1)
        from_high = grp_rim(packs[3], -1)
        extended = jnp.concatenate([state_bf, from_left, from_right, from_low, from_high], axis=0)
        gathered = jnp.dot(
            column_select,
            extended.reshape(ext_count, flat_width),
            preferred_element_type=jnp.float32,
        ).astype(jnp.bfloat16)
        gathered = gathered.reshape(tile_count, stored, vectors_count, tile_rows)
        return jnp.einsum("tkij,tkrj->tri", jacobian, gathered, preferred_element_type=jnp.float32)

    def jacobi(vectors):
        return jnp.einsum(
            "tij,trj->tri",
            smoother,
            vectors.astype(jnp.bfloat16),
            preferred_element_type=jnp.float32,
        )

    position = lax.axis_index("dev")
    mine = lax.dynamic_slice_in_dim(owner[:, 0], position * blocks, blocks)
    order = jnp.arange(blocks, dtype=jnp.int32)
    earlier = (mine[:, None] == mine[None, :]) & (order[None, :] < order[:, None])
    slot = jnp.sum(earlier.astype(jnp.int32), axis=1)
    fetched = lax.all_to_all(coarse_inverse[0], "dev", split_axis=0, concat_axis=0, tiled=True)
    picked = fetched[mine, slot]
    state = OMEGA * jacobi(rhs)
    for sweep in range(SWEEPS - 1):
        state = state + OMEGA * jacobi(rhs - operate(state))
    residual = rhs - operate(state)
    restricted = jnp.einsum(
        "tij,trj->tri",
        restriction,
        residual.astype(jnp.bfloat16),
        preferred_element_type=jnp.float32,
    )
    partial_sum = restricted.reshape(blocks, AGG, vectors_count, tile_rows).sum(axis=1)
    groups = lax.axis_size("grp")
    group = lax.axis_index("grp")
    share = blocks // groups
    quarters = partial_sum.astype(jnp.bfloat16).reshape(groups, share, vectors_count, tile_rows)
    total = quarters[group].astype(jnp.float32)
    for by in range(1, groups):
        pairs = [(i, (i + by) % groups) for i in range(groups)]
        total = total + lax.ppermute(quarters[(group + by) % groups], "grp", pairs).astype(jnp.float32)
    coarse = total.astype(jnp.bfloat16)
    picked_share = lax.dynamic_slice_in_dim(picked, group * share, share)
    solved = jnp.einsum("cab,crb->cra", picked_share, coarse, preferred_element_type=jnp.float32)
    fix_share = solved.astype(jnp.bfloat16)
    pieces = [fix_share]
    for by in range(1, groups):
        pairs = [(i, (i + by) % groups) for i in range(groups)]
        pieces.append(lax.ppermute(fix_share, "grp", pairs))
    stacked = jnp.stack(pieces)
    order = (group - jnp.arange(groups, dtype=jnp.int32)) % groups
    coarse_fix = jnp.take(stacked, order, axis=0).reshape(blocks, vectors_count, tile_rows)
    fine_fix = jnp.repeat(coarse_fix, AGG, axis=0)
    state = state + jnp.einsum(
        "tji,trj->tri", restriction, fine_fix, preferred_element_type=jnp.float32
    )
    for sweep in range(SWEEPS):
        state = state + OMEGA * jacobi(rhs - operate(state))
    return state


def solution(mesh):
    in_specs = (
        P(("grp", "dev"), None, None),
        P(("grp", "dev"), None, None, None),
        P(("grp", "dev"), None),
        P(("grp", "dev"), None, None),
        P(("grp", "dev"), None, None),
        P(("grp", "dev"), None, None),
        P("dev", None, None, None, None),
        P(),
    )
    out_specs = P(("grp", "dev"), None, None)
    return jax.shard_map(shards, mesh=mesh, in_specs=in_specs, out_specs=out_specs, check_vma=False)
```

```python
import jax
import jax.numpy as jnp
from jax import lax
from jax.sharding import PartitionSpec as P

AGG = 2
SWEEPS = 3


OMEGA = 0.8


def shifted(value, axis, by):
    length = lax.axis_size(axis)
    pairs = [(i, i + by) for i in range(length) if 0 <= i + by < length]
    return lax.ppermute(value, axis, pairs)


def dev_rim(pack, offset):
    return shifted(pack, "dev", offset)


def grp_rim(pack, offset):
    return shifted(pack, "grp", offset)


def shards(rhs, jacobian, columns, send_tiles, smoother, restriction, coarse_inverse, owner):
    tile_count = rhs.shape[0]
    vectors_count = rhs.shape[1]
    tile_rows = rhs.shape[2]
    stored = columns.shape[1]
    blocks = tile_count // AGG
    listed = send_tiles[0]
    rim_count = listed.shape[1]
    ext_count = tile_count + 4 * rim_count
    flat_width = vectors_count * tile_rows
    ext_range = jnp.arange(ext_count, dtype=jnp.int32)
    column_flat = columns.reshape(-1)
    own_range = jnp.arange(tile_count, dtype=jnp.int32)
    rim_select = (listed.reshape(-1)[:, None] == own_range[None, :]).astype(jnp.bfloat16)

    def operate(state):
        state_bf = state.astype(jnp.bfloat16)
        state_flat = state_bf.reshape(tile_count, flat_width)
        packs = jnp.dot(rim_select, state_flat, preferred_element_type=jnp.float32).astype(
            jnp.bfloat16
        )
        packs = packs.reshape(4, rim_count, vectors_count, tile_rows)
        from_left = dev_rim(packs[0], 1)
        from_right = dev_rim(packs[1], -1)
        from_low = grp_rim(packs[2], 1)
        from_high = grp_rim(packs[3], -1)
        extended = jnp.concatenate([state_bf, from_left, from_right, from_low, from_high], axis=0)
        gathered = jnp.take(extended, column_flat, axis=0, mode="clip")
        gathered = lax.optimization_barrier(gathered)
        gathered = gathered.reshape(tile_count, stored, vectors_count, tile_rows)
        return jnp.einsum("tkij,tkrj->tri", jacobian, gathered, preferred_element_type=jnp.float32)

    def jacobi(vectors):
        return jnp.einsum(
            "tij,trj->tri",
            smoother,
            vectors.astype(jnp.bfloat16),
            preferred_element_type=jnp.float32,
        )

    position = lax.axis_index("dev")
    mine = lax.dynamic_slice_in_dim(owner[:, 0], position * blocks, blocks)
    order = jnp.arange(blocks, dtype=jnp.int32)
    earlier = (mine[:, None] == mine[None, :]) & (order[None, :] < order[:, None])
    slot = jnp.sum(earlier.astype(jnp.int32), axis=1)
    fetched = lax.all_to_all(coarse_inverse[0], "dev", split_axis=0, concat_axis=0, tiled=True)
    picked = fetched[mine, slot]
    state = OMEGA * jacobi(rhs)
    for sweep in range(SWEEPS - 1):
        state = state + OMEGA * jacobi(rhs - operate(state))
    residual = rhs - operate(state)
    restricted = jnp.einsum(
        "tij,trj->tri",
        restriction,
        residual.astype(jnp.bfloat16),
        preferred_element_type=jnp.float32,
    )
    partial_sum = restricted.reshape(blocks, AGG, vectors_count, tile_rows).sum(axis=1)
    groups = lax.axis_size("grp")
    group = lax.axis_index("grp")
    share = blocks // groups
    quarters = partial_sum.astype(jnp.bfloat16).reshape(groups, share, vectors_count, tile_rows)
    total = quarters[group].astype(jnp.float32)
    for by in range(1, groups):
        pairs = [(i, (i + by) % groups) for i in range(groups)]
        total = total + lax.ppermute(quarters[(group + by) % groups], "grp", pairs).astype(jnp.float32)
    coarse = total.astype(jnp.bfloat16)
    picked_share = lax.dynamic_slice_in_dim(picked, group * share, share)
    solved = jnp.einsum("cab,crb->cra", picked_share, coarse, preferred_element_type=jnp.float32)
    fix_share = solved.astype(jnp.bfloat16)
    pieces = [fix_share]
    for by in range(1, groups):
        pairs = [(i, (i + by) % groups) for i in range(groups)]
        pieces.append(lax.ppermute(fix_share, "grp", pairs))
    stacked = jnp.stack(pieces)
    order = (group - jnp.arange(groups, dtype=jnp.int32)) % groups
    coarse_fix = jnp.take(stacked, order, axis=0).reshape(blocks, vectors_count, tile_rows)
    fine_fix = jnp.repeat(coarse_fix, AGG, axis=0)
    state = state + jnp.einsum(
        "tji,trj->tri", restriction, fine_fix, preferred_element_type=jnp.float32
    )
    for sweep in range(SWEEPS):
        state = state + OMEGA * jacobi(rhs - operate(state))
    return state


def solution(mesh):
    in_specs = (
        P(("grp", "dev"), None, None),
        P(("grp", "dev"), None, None, None),
        P(("grp", "dev"), None),
        P(("grp", "dev"), None, None),
        P(("grp", "dev"), None, None),
        P(("grp", "dev"), None, None),
        P("dev", None, None, None, None),
        P(),
    )
    out_specs = P(("grp", "dev"), None, None)
    return jax.shard_map(shards, mesh=mesh, in_specs=in_specs, out_specs=out_specs, check_vma=False)
```

```python
import jax
import jax.numpy as jnp
from jax import lax
from jax.sharding import PartitionSpec as P

AGG = 2
SWEEPS = 3


OMEGA = 0.8


def shifted(value, axis, by):
    length = lax.axis_size(axis)
    pairs = [(i, i + by) for i in range(length) if 0 <= i + by < length]
    return lax.ppermute(value, axis, pairs)


def dev_rim(pack, offset):
    return shifted(pack, "dev", offset)


def grp_rim(pack, offset):
    return shifted(pack, "grp", offset)


def shards(rhs, jacobian, columns, send_tiles, smoother, restriction, coarse_inverse, owner):
    tile_count = rhs.shape[0]
    vectors_count = rhs.shape[1]
    tile_rows = rhs.shape[2]
    stored = columns.shape[1]
    blocks = tile_count // AGG
    listed = send_tiles[0]
    rim_count = listed.shape[1]
    ext_count = tile_count + 4 * rim_count
    flat_width = vectors_count * tile_rows
    ext_range = jnp.arange(ext_count, dtype=jnp.int32)
    own_select = (columns.reshape(-1)[:, None] == ext_range[None, :tile_count]).astype(jnp.bfloat16)
    rim_pick = (columns.reshape(-1)[:, None] == ext_range[None, tile_count:]).astype(jnp.bfloat16)
    own_range = jnp.arange(tile_count, dtype=jnp.int32)
    rim_select = (listed.reshape(-1)[:, None] == own_range[None, :]).astype(jnp.bfloat16)

    def operate(state):
        state_bf = state.astype(jnp.bfloat16)
        state_flat = state_bf.reshape(tile_count, flat_width)
        packs = jnp.dot(rim_select, state_flat, preferred_element_type=jnp.float32).astype(
            jnp.bfloat16
        )
        packs = packs.reshape(4, rim_count, vectors_count, tile_rows)
        from_left = dev_rim(packs[0], 1)
        from_right = dev_rim(packs[1], -1)
        from_low = grp_rim(packs[2], 1)
        from_high = grp_rim(packs[3], -1)
        near = jnp.dot(own_select, state_flat, preferred_element_type=jnp.float32).astype(jnp.bfloat16)
        near = lax.optimization_barrier(near)
        rims = jnp.concatenate([from_left, from_right, from_low, from_high], axis=0)
        far = jnp.dot(
            rim_pick,
            rims.reshape(4 * rim_count, flat_width),
            preferred_element_type=jnp.float32,
        ).astype(jnp.bfloat16)
        gathered = near + far
        gathered = gathered.reshape(tile_count, stored, vectors_count, tile_rows)
        return jnp.einsum("tkij,tkrj->tri", jacobian, gathered, preferred_element_type=jnp.float32)

    def jacobi(vectors):
        return jnp.einsum(
            "tij,trj->tri",
            smoother,
            vectors.astype(jnp.bfloat16),
            preferred_element_type=jnp.float32,
        )

    position = lax.axis_index("dev")
    mine = lax.dynamic_slice_in_dim(owner[:, 0], position * blocks, blocks)
    order = jnp.arange(blocks, dtype=jnp.int32)
    earlier = (mine[:, None] == mine[None, :]) & (order[None, :] < order[:, None])
    slot = jnp.sum(earlier.astype(jnp.int32), axis=1)
    fetched = lax.all_to_all(coarse_inverse[0], "dev", split_axis=0, concat_axis=0, tiled=True)
    picked = fetched[mine, slot]
    state = OMEGA * jacobi(rhs)
    for sweep in range(SWEEPS - 1):
        state = state + OMEGA * jacobi(rhs - operate(state))
    residual = rhs - operate(state)
    restricted = jnp.einsum(
        "tij,trj->tri",
        restriction,
        residual.astype(jnp.bfloat16),
        preferred_element_type=jnp.float32,
    )
    partial_sum = restricted.reshape(blocks, AGG, vectors_count, tile_rows).sum(axis=1)
    groups = lax.axis_size("grp")
    group = lax.axis_index("grp")
    share = blocks // groups
    quarters = partial_sum.astype(jnp.bfloat16).reshape(groups, share, vectors_count, tile_rows)
    total = quarters[group].astype(jnp.float32)
    for by in range(1, groups):
        pairs = [(i, (i + by) % groups) for i in range(groups)]
        total = total + lax.ppermute(quarters[(group + by) % groups], "grp", pairs).astype(jnp.float32)
    coarse = total.astype(jnp.bfloat16)
    picked_share = lax.dynamic_slice_in_dim(picked, group * share, share)
    solved = jnp.einsum("cab,crb->cra", picked_share, coarse, preferred_element_type=jnp.float32)
    fix_share = solved.astype(jnp.bfloat16)
    pieces = [fix_share]
    for by in range(1, groups):
        pairs = [(i, (i + by) % groups) for i in range(groups)]
        pieces.append(lax.ppermute(fix_share, "grp", pairs))
    stacked = jnp.stack(pieces)
    order = (group - jnp.arange(groups, dtype=jnp.int32)) % groups
    coarse_fix = jnp.take(stacked, order, axis=0).reshape(blocks, vectors_count, tile_rows)
    fine_fix = jnp.repeat(coarse_fix, AGG, axis=0)
    state = state + jnp.einsum(
        "tji,trj->tri", restriction, fine_fix, preferred_element_type=jnp.float32
    )
    for sweep in range(SWEEPS):
        state = state + OMEGA * jacobi(rhs - operate(state))
    return state


def solution(mesh):
    in_specs = (
        P(("grp", "dev"), None, None),
        P(("grp", "dev"), None, None, None),
        P(("grp", "dev"), None),
        P(("grp", "dev"), None, None),
        P(("grp", "dev"), None, None),
        P(("grp", "dev"), None, None),
        P("dev", None, None, None, None),
        P(),
    )
    out_specs = P(("grp", "dev"), None, None)
    return jax.shard_map(shards, mesh=mesh, in_specs=in_specs, out_specs=out_specs, check_vma=False)
```

```python
import jax
import jax.numpy as jnp
from jax import lax
from jax.sharding import PartitionSpec as P

AGG = 2
SWEEPS = 3


OMEGA = 0.8


def shifted(value, axis, by):
    length = lax.axis_size(axis)
    pairs = [(i, i + by) for i in range(length) if 0 <= i + by < length]
    return lax.ppermute(value, axis, pairs)


def dev_rim(pack, offset):
    return shifted(pack, "dev", offset)


def grp_rim(pack, offset):
    return shifted(pack, "grp", offset)


def shards(rhs, jacobian, columns, send_tiles, smoother, restriction, coarse_inverse, owner):
    tile_count = rhs.shape[0]
    vectors_count = rhs.shape[1]
    tile_rows = rhs.shape[2]
    stored = columns.shape[1]
    blocks = tile_count // AGG
    listed = send_tiles[0]
    rim_count = listed.shape[1]
    ext_count = tile_count + 4 * rim_count
    flat_width = vectors_count * tile_rows
    ext_range = jnp.arange(ext_count, dtype=jnp.int32)
    column_select = (columns.reshape(-1)[:, None] == ext_range[None, :]).astype(jnp.bfloat16)
    own_range = jnp.arange(tile_count, dtype=jnp.int32)
    rim_select = [(listed[j][:, None] == own_range[None, :]).astype(jnp.bfloat16) for j in range(4)]

    def operate(state):
        state_bf = state.astype(jnp.bfloat16)
        state_flat = state_bf.reshape(tile_count, flat_width)
        packs = [
            jnp.dot(pick, state_flat, preferred_element_type=jnp.float32)
            .astype(jnp.bfloat16)
            .reshape(rim_count, vectors_count, tile_rows)
            for pick in rim_select
        ]
        from_left = dev_rim(packs[0], 1)
        from_right = dev_rim(packs[1], -1)
        from_low = grp_rim(packs[2], 1)
        from_high = grp_rim(packs[3], -1)
        extended = jnp.concatenate([state_bf, from_left, from_right, from_low, from_high], axis=0)
        gathered = jnp.dot(
            column_select,
            extended.reshape(ext_count, flat_width),
            preferred_element_type=jnp.float32,
        ).astype(jnp.bfloat16)
        gathered = gathered.reshape(tile_count, stored, vectors_count, tile_rows)
        return jnp.einsum("tkij,tkrj->tri", jacobian, gathered, preferred_element_type=jnp.float32)

    def jacobi(vectors):
        return jnp.einsum(
            "tij,trj->tri",
            smoother,
            vectors.astype(jnp.bfloat16),
            preferred_element_type=jnp.float32,
        )

    position = lax.axis_index("dev")
    mine = lax.dynamic_slice_in_dim(owner[:, 0], position * blocks, blocks)
    order = jnp.arange(blocks, dtype=jnp.int32)
    earlier = (mine[:, None] == mine[None, :]) & (order[None, :] < order[:, None])
    slot = jnp.sum(earlier.astype(jnp.int32), axis=1)
    fetched = lax.all_to_all(coarse_inverse[0], "dev", split_axis=0, concat_axis=0, tiled=True)
    state = OMEGA * jacobi(rhs)
    for sweep in range(SWEEPS - 1):
        state = state + OMEGA * jacobi(rhs - operate(state))
    residual = rhs - operate(state)
    restricted = jnp.einsum(
        "tij,trj->tri",
        restriction,
        residual.astype(jnp.bfloat16),
        preferred_element_type=jnp.float32,
    )
    partial_sum = restricted.reshape(blocks, AGG, vectors_count, tile_rows).sum(axis=1)
    groups = lax.axis_size("grp")
    group = lax.axis_index("grp")
    share = blocks // groups
    quarters = partial_sum.astype(jnp.bfloat16).reshape(groups, share, vectors_count, tile_rows)
    total = quarters[group].astype(jnp.float32)
    for by in range(1, groups):
        pairs = [(i, (i + by) % groups) for i in range(groups)]
        total = total + lax.ppermute(quarters[(group + by) % groups], "grp", pairs).astype(jnp.float32)
    coarse = total.astype(jnp.bfloat16)
    mine_share = lax.dynamic_slice_in_dim(mine, group * share, share)
    slot_share = lax.dynamic_slice_in_dim(slot, group * share, share)
    picked_share = fetched[mine_share, slot_share]
    solved = jnp.einsum("cab,crb->cra", picked_share, coarse, preferred_element_type=jnp.float32)
    fix_share = solved.astype(jnp.bfloat16)
    pieces = [fix_share]
    for by in range(1, groups):
        pairs = [(i, (i + by) % groups) for i in range(groups)]
        pieces.append(lax.ppermute(fix_share, "grp", pairs))
    stacked = jnp.stack(pieces)
    order = (group - jnp.arange(groups, dtype=jnp.int32)) % groups
    coarse_fix = jnp.take(stacked, order, axis=0).reshape(blocks, vectors_count, tile_rows)
    fine_fix = jnp.repeat(coarse_fix, AGG, axis=0)
    state = state + jnp.einsum(
        "tji,trj->tri", restriction, fine_fix, preferred_element_type=jnp.float32
    )
    for sweep in range(SWEEPS):
        state = state + OMEGA * jacobi(rhs - operate(state))
    return state


def solution(mesh):
    in_specs = (
        P(("grp", "dev"), None, None),
        P(("grp", "dev"), None, None, None),
        P(("grp", "dev"), None),
        P(("grp", "dev"), None, None),
        P(("grp", "dev"), None, None),
        P(("grp", "dev"), None, None),
        P("dev", None, None, None, None),
        P(),
    )
    out_specs = P(("grp", "dev"), None, None)
    return jax.shard_map(shards, mesh=mesh, in_specs=in_specs, out_specs=out_specs, check_vma=False)
```

```python
import jax
import jax.numpy as jnp
from jax import lax
from jax.sharding import PartitionSpec as P

AGG = 2
SWEEPS = 3


OMEGA = 0.8


def shifted(value, axis, by):
    length = lax.axis_size(axis)
    pairs = [(i, i + by) for i in range(length) if 0 <= i + by < length]
    return lax.ppermute(value, axis, pairs)


def dev_rim(pack, offset):
    return shifted(pack, "dev", offset)


def grp_rim(pack, offset):
    return shifted(pack, "grp", offset)


def shards(rhs, jacobian, columns, send_tiles, smoother, restriction, coarse_inverse, owner):
    tile_count = rhs.shape[0]
    vectors_count = rhs.shape[1]
    tile_rows = rhs.shape[2]
    stored = columns.shape[1]
    blocks = tile_count // AGG
    listed = send_tiles[0]
    rim_count = listed.shape[1]
    ext_count = tile_count + 4 * rim_count
    flat_width = vectors_count * tile_rows
    ext_range = jnp.arange(ext_count, dtype=jnp.int32)
    column_select = (columns.reshape(-1)[:, None] == ext_range[None, :]).astype(jnp.bfloat16)
    own_range = jnp.arange(tile_count, dtype=jnp.int32)
    rim_select = (listed.reshape(-1)[:, None] == own_range[None, :]).astype(jnp.bfloat16)

    def operate(state):
        state_bf = state.astype(jnp.bfloat16)
        state_flat = state_bf.reshape(tile_count, flat_width)
        packs = jnp.dot(rim_select, state_flat, preferred_element_type=jnp.float32).astype(
            jnp.bfloat16
        )
        packs = packs.reshape(4, rim_count, vectors_count, tile_rows)
        from_left = dev_rim(packs[0], 1)
        from_right = dev_rim(packs[1], -1)
        from_low = grp_rim(packs[2], 1)
        from_high = grp_rim(packs[3], -1)
        extended = jnp.concatenate([state_bf, from_left, from_right, from_low, from_high], axis=0)
        gathered = jnp.dot(
            column_select,
            extended.reshape(ext_count, flat_width),
            preferred_element_type=jnp.float32,
        ).astype(jnp.bfloat16)
        gathered = gathered.reshape(tile_count, stored, vectors_count, tile_rows)
        return jnp.einsum("tkij,tkrj->tri", jacobian, gathered, preferred_element_type=jnp.float32)

    def jacobi(vectors):
        return jnp.einsum(
            "tij,trj->tri",
            smoother,
            vectors.astype(jnp.bfloat16),
            preferred_element_type=jnp.float32,
        )

    position = lax.axis_index("dev")
    mine = lax.dynamic_slice_in_dim(owner[:, 0], position * blocks, blocks)
    order = jnp.arange(blocks, dtype=jnp.int32)
    earlier = (mine[:, None] == mine[None, :]) & (order[None, :] < order[:, None])
    slot = jnp.sum(earlier.astype(jnp.int32), axis=1)
    fetched = lax.all_to_all(coarse_inverse[0], "dev", split_axis=0, concat_axis=0, tiled=True)
    state = OMEGA * jacobi(rhs)
    def sweep(index, state):
        return state + OMEGA * jacobi(rhs - operate(state))

    state = lax.fori_loop(0, SWEEPS - 1, sweep, state)
    residual = rhs - operate(state)
    restricted = jnp.einsum(
        "tij,trj->tri",
        restriction,
        residual.astype(jnp.bfloat16),
        preferred_element_type=jnp.float32,
    )
    partial_sum = restricted.reshape(blocks, AGG, vectors_count, tile_rows).sum(axis=1)
    groups = lax.axis_size("grp")
    group = lax.axis_index("grp")
    share = blocks // groups
    quarters = partial_sum.astype(jnp.bfloat16).reshape(groups, share, vectors_count, tile_rows)
    total = quarters[group].astype(jnp.float32)
    for by in range(1, groups):
        pairs = [(i, (i + by) % groups) for i in range(groups)]
        total = total + lax.ppermute(quarters[(group + by) % groups], "grp", pairs).astype(jnp.float32)
    coarse = total.astype(jnp.bfloat16)
    mine_share = lax.dynamic_slice_in_dim(mine, group * share, share)
    slot_share = lax.dynamic_slice_in_dim(slot, group * share, share)
    picked_share = fetched[mine_share, slot_share]
    solved = jnp.einsum("cab,crb->cra", picked_share, coarse, preferred_element_type=jnp.float32)
    fix_share = solved.astype(jnp.bfloat16)
    pieces = [fix_share]
    for by in range(1, groups):
        pairs = [(i, (i + by) % groups) for i in range(groups)]
        pieces.append(lax.ppermute(fix_share, "grp", pairs))
    stacked = jnp.stack(pieces)
    order = (group - jnp.arange(groups, dtype=jnp.int32)) % groups
    coarse_fix = jnp.take(stacked, order, axis=0).reshape(blocks, vectors_count, tile_rows)
    fine_fix = jnp.repeat(coarse_fix, AGG, axis=0)
    state = state + jnp.einsum(
        "tji,trj->tri", restriction, fine_fix, preferred_element_type=jnp.float32
    )
    state = lax.fori_loop(0, SWEEPS, sweep, state)
    return state


def solution(mesh):
    in_specs = (
        P(("grp", "dev"), None, None),
        P(("grp", "dev"), None, None, None),
        P(("grp", "dev"), None),
        P(("grp", "dev"), None, None),
        P(("grp", "dev"), None, None),
        P(("grp", "dev"), None, None),
        P("dev", None, None, None, None),
        P(),
    )
    out_specs = P(("grp", "dev"), None, None)
    return jax.shard_map(shards, mesh=mesh, in_specs=in_specs, out_specs=out_specs, check_vma=False)
```

```python
import jax
import jax.numpy as jnp
from jax import lax
from jax.sharding import PartitionSpec as P

AGG = 2
SWEEPS = 3


OMEGA = 0.8


def shifted(value, axis, by):
    length = lax.axis_size(axis)
    pairs = [(i, i + by) for i in range(length) if 0 <= i + by < length]
    return lax.ppermute(value, axis, pairs)


def dev_rim(pack, offset):
    return shifted(pack, "dev", offset)


def grp_rim(pack, offset):
    return shifted(pack, "grp", offset)


def shards(rhs, jacobian, columns, send_tiles, smoother, restriction, coarse_inverse, owner):
    tile_count = rhs.shape[0]
    vectors_count = rhs.shape[1]
    tile_rows = rhs.shape[2]
    stored = columns.shape[1]
    blocks = tile_count // AGG
    listed = send_tiles[0]
    rim_count = listed.shape[1]
    ext_count = tile_count + 4 * rim_count
    flat_width = vectors_count * tile_rows
    ext_range = jnp.arange(ext_count, dtype=jnp.int32)
    column_select = (columns.reshape(-1)[:, None] == ext_range[None, :]).astype(jnp.bfloat16)
    own_range = jnp.arange(tile_count, dtype=jnp.int32)
    rim_select = (listed.reshape(-1)[:, None] == own_range[None, :]).astype(jnp.bfloat16)

    def operate(state):
        state_bf = state.astype(jnp.bfloat16)
        state_flat = state_bf.reshape(tile_count, flat_width)
        packs = jnp.dot(rim_select, state_flat, preferred_element_type=jnp.float32).astype(
            jnp.bfloat16
        )
        packs = packs.reshape(4, rim_count, vectors_count, tile_rows)
        from_left = dev_rim(packs[0], 1)
        from_right = dev_rim(packs[1], -1)
        from_low = grp_rim(packs[2], 1)
        from_high = grp_rim(packs[3], -1)
        extended = jnp.concatenate([state_bf, from_left, from_right, from_low, from_high], axis=0)
        gathered = jnp.dot(
            column_select,
            extended.reshape(ext_count, flat_width),
            preferred_element_type=jnp.float32,
        ).astype(jnp.bfloat16)
        gathered = gathered.reshape(tile_count, stored, vectors_count, tile_rows)
        return jnp.einsum("tkij,tkrj->tri", jacobian, gathered, preferred_element_type=jnp.float32)

    def jacobi(vectors):
        return jnp.einsum(
            "tij,trj->tri",
            smoother,
            vectors.astype(jnp.bfloat16),
            preferred_element_type=jnp.float32,
        )

    position = lax.axis_index("dev")
    mine = lax.dynamic_slice_in_dim(owner[:, 0], position * blocks, blocks)
    order = jnp.arange(blocks, dtype=jnp.int32)
    earlier = (mine[:, None] == mine[None, :]) & (order[None, :] < order[:, None])
    slot = jnp.sum(earlier.astype(jnp.int32), axis=1)
    fetched = lax.all_to_all(coarse_inverse[0], "dev", split_axis=0, concat_axis=0, tiled=True)
    state = OMEGA * jacobi(rhs)
    for sweep in range(SWEEPS - 1):
        state = state + OMEGA * jacobi(rhs - operate(state))
    residual = rhs - operate(state)
    restricted = jnp.einsum(
        "tij,trj->tri",
        restriction,
        residual.astype(jnp.bfloat16),
        preferred_element_type=jnp.float32,
    )
    partial_sum = restricted.reshape(blocks, AGG, vectors_count, tile_rows).sum(axis=1)
    groups = lax.axis_size("grp")
    group = lax.axis_index("grp")
    share = blocks // groups
    quarters = partial_sum.astype(jnp.bfloat16).reshape(groups, share, vectors_count, tile_rows)
    total = quarters[group].astype(jnp.float32)
    for by in range(1, groups):
        pairs = [(i, (i + by) % groups) for i in range(groups)]
        total = total + lax.ppermute(quarters[(group + by) % groups], "grp", pairs).astype(jnp.float32)
    coarse = total.astype(jnp.bfloat16)
    mine_share = lax.dynamic_slice_in_dim(mine, group * share, share)
    slot_share = lax.dynamic_slice_in_dim(slot, group * share, share)
    picked_share = fetched[mine_share, slot_share]
    solved = jnp.einsum("cab,crb->cra", picked_share, coarse, preferred_element_type=jnp.float32)
    fix_share = solved.astype(jnp.bfloat16)
    pieces = [fix_share]
    for by in range(1, groups):
        pairs = [(i, (i + by) % groups) for i in range(groups)]
        pieces.append(lax.ppermute(fix_share, "grp", pairs))
    stacked = jnp.stack(pieces)
    order = (group - jnp.arange(groups, dtype=jnp.int32)) % groups
    coarse_fix = jnp.take(stacked, order, axis=0).reshape(blocks, vectors_count, tile_rows)
    fine_fix = jnp.repeat(coarse_fix, AGG, axis=0)
    state = state + jnp.einsum(
        "tji,trj->tri", restriction, fine_fix, preferred_element_type=jnp.float32
    )
    for sweep in range(SWEEPS):
        state = state + OMEGA * jacobi(rhs - operate(state))
    return state


def solution(mesh):
    in_specs = (
        P(("grp", "dev"), None, None),
        P(("grp", "dev"), None, None, None),
        P(("grp", "dev"), None),
        P(("grp", "dev"), None, None),
        P(("grp", "dev"), None, None),
        P(("grp", "dev"), None, None),
        P("dev", None, None, None, None),
        P(),
    )
    out_specs = P(("grp", "dev"), None, None)
    return jax.shard_map(shards, mesh=mesh, in_specs=in_specs, out_specs=out_specs, check_vma=False)
```

```python
import jax
import jax.numpy as jnp
from jax import lax
from jax.sharding import PartitionSpec as P

AGG = 2
SWEEPS = 3


OMEGA = 0.8


def shifted(value, axis, by):
    length = lax.axis_size(axis)
    pairs = [(i, i + by) for i in range(length) if 0 <= i + by < length]
    return lax.ppermute(value, axis, pairs)


def dev_rim(pack, offset):
    return shifted(pack, "dev", offset)


def grp_rim(pack, offset):
    return shifted(pack, "grp", offset)


def shards(rhs, jacobian, columns, send_tiles, smoother, restriction, coarse_inverse, owner):
    tile_count = rhs.shape[0]
    vectors_count = rhs.shape[1]
    tile_rows = rhs.shape[2]
    stored = columns.shape[1]
    blocks = tile_count // AGG
    listed = send_tiles[0]
    rim_count = listed.shape[1]
    ext_count = tile_count + 4 * rim_count
    flat_width = vectors_count * tile_rows
    ext_range = jnp.arange(ext_count, dtype=jnp.int32)
    column_select = (columns.reshape(-1)[:, None] == ext_range[None, :]).astype(jnp.bfloat16)
    own_range = jnp.arange(tile_count, dtype=jnp.int32)
    rim_select = (listed.reshape(-1)[:, None] == own_range[None, :]).astype(jnp.bfloat16)

    def gather(state):
        state_bf = state.astype(jnp.bfloat16)
        state_flat = state_bf.reshape(tile_count, flat_width)
        packs = jnp.dot(rim_select, state_flat, preferred_element_type=jnp.float32).astype(
            jnp.bfloat16
        )
        packs = packs.reshape(4, rim_count, vectors_count, tile_rows)
        from_left = dev_rim(packs[0], 1)
        from_right = dev_rim(packs[1], -1)
        from_low = grp_rim(packs[2], 1)
        from_high = grp_rim(packs[3], -1)
        extended = jnp.concatenate([state_bf, from_left, from_right, from_low, from_high], axis=0)
        gathered = jnp.dot(
            column_select,
            extended.reshape(ext_count, flat_width),
            preferred_element_type=jnp.float32,
        ).astype(jnp.bfloat16)
        return gathered.reshape(tile_count, stored, vectors_count, tile_rows)

    def operate(state):
        return jnp.einsum("tkij,tkrj->tri", jacobian, gather(state), preferred_element_type=jnp.float32)

    def jacobi(vectors):
        return jnp.einsum(
            "tij,trj->tri",
            smoother,
            vectors.astype(jnp.bfloat16),
            preferred_element_type=jnp.float32,
        )

    position = lax.axis_index("dev")
    mine = lax.dynamic_slice_in_dim(owner[:, 0], position * blocks, blocks)
    order = jnp.arange(blocks, dtype=jnp.int32)
    earlier = (mine[:, None] == mine[None, :]) & (order[None, :] < order[:, None])
    slot = jnp.sum(earlier.astype(jnp.int32), axis=1)
    fetched = lax.all_to_all(coarse_inverse[0], "dev", split_axis=0, concat_axis=0, tiled=True)
    state = OMEGA * jacobi(rhs)
    for sweep in range(SWEEPS - 1):
        state = state + OMEGA * jacobi(rhs - operate(state))
    groups = lax.axis_size("grp")
    group = lax.axis_index("grp")
    share = blocks // groups
    span = tile_count // groups
    gathered = gather(state)
    total = None
    for by in list(range(1, groups)) + [0]:
        part = (group + by) % groups
        start = part * span
        near = lax.dynamic_slice_in_dim(gathered, start, span)
        tiles = lax.dynamic_slice_in_dim(jacobian, start, span)
        residual = lax.dynamic_slice_in_dim(rhs, start, span) - jnp.einsum(
            "tkij,tkrj->tri", tiles, near, preferred_element_type=jnp.float32
        )
        restricted = jnp.einsum(
            "tij,trj->tri",
            lax.dynamic_slice_in_dim(restriction, start, span),
            residual.astype(jnp.bfloat16),
            preferred_element_type=jnp.float32,
        )
        piece = restricted.reshape(share, AGG, vectors_count, tile_rows).sum(axis=1).astype(jnp.bfloat16)
        if by:
            pairs = [(i, (i + by) % groups) for i in range(groups)]
            piece = lax.ppermute(piece, "grp", pairs)
        total = piece.astype(jnp.float32) if total is None else total + piece.astype(jnp.float32)
    coarse = total.astype(jnp.bfloat16)
    mine_share = lax.dynamic_slice_in_dim(mine, group * share, share)
    slot_share = lax.dynamic_slice_in_dim(slot, group * share, share)
    picked_share = fetched[mine_share, slot_share]
    solved = jnp.einsum("cab,crb->cra", picked_share, coarse, preferred_element_type=jnp.float32)
    fix_share = solved.astype(jnp.bfloat16)
    pieces = [fix_share]
    for by in range(1, groups):
        pairs = [(i, (i + by) % groups) for i in range(groups)]
        pieces.append(lax.ppermute(fix_share, "grp", pairs))
    stacked = jnp.stack(pieces)
    order = (group - jnp.arange(groups, dtype=jnp.int32)) % groups
    coarse_fix = jnp.take(stacked, order, axis=0).reshape(blocks, vectors_count, tile_rows)
    fine_fix = jnp.repeat(coarse_fix, AGG, axis=0)
    state = state + jnp.einsum(
        "tji,trj->tri", restriction, fine_fix, preferred_element_type=jnp.float32
    )
    for sweep in range(SWEEPS):
        state = state + OMEGA * jacobi(rhs - operate(state))
    return state


def solution(mesh):
    in_specs = (
        P(("grp", "dev"), None, None),
        P(("grp", "dev"), None, None, None),
        P(("grp", "dev"), None),
        P(("grp", "dev"), None, None),
        P(("grp", "dev"), None, None),
        P(("grp", "dev"), None, None),
        P("dev", None, None, None, None),
        P(),
    )
    out_specs = P(("grp", "dev"), None, None)
    return jax.shard_map(shards, mesh=mesh, in_specs=in_specs, out_specs=out_specs, check_vma=False)
```

```python
import jax
import jax.numpy as jnp
from jax import lax
from jax.sharding import PartitionSpec as P

AGG = 2
SWEEPS = 3


OMEGA = 0.8


def shifted(value, axis, by):
    length = lax.axis_size(axis)
    pairs = [(i, i + by) for i in range(length) if 0 <= i + by < length]
    return lax.ppermute(value, axis, pairs)


def dev_rim(pack, offset):
    return shifted(pack, "dev", offset)


def grp_rim(pack, offset):
    return shifted(pack, "grp", offset)


def shards(rhs, jacobian, columns, send_tiles, smoother, restriction, coarse_inverse, owner):
    tile_count = rhs.shape[0]
    vectors_count = rhs.shape[1]
    tile_rows = rhs.shape[2]
    stored = columns.shape[1]
    blocks = tile_count // AGG
    listed = send_tiles[0]
    rim_count = listed.shape[1]
    ext_count = tile_count + 4 * rim_count
    flat_width = vectors_count * tile_rows
    ext_range = jnp.arange(ext_count, dtype=jnp.int32)
    column_select = (columns.reshape(-1)[:, None] == ext_range[None, :]).astype(jnp.bfloat16)
    own_range = jnp.arange(tile_count, dtype=jnp.int32)
    rim_select = (listed.reshape(-1)[:, None] == own_range[None, :]).astype(jnp.bfloat16)

    def operate(state, packs=None):
        state_bf = state.astype(jnp.bfloat16)
        state_flat = state_bf.reshape(tile_count, flat_width)
        if packs is None:
            packs = jnp.dot(rim_select, state_flat, preferred_element_type=jnp.float32).astype(
                jnp.bfloat16
            )
        packs = packs.reshape(4, rim_count, vectors_count, tile_rows)
        from_left = dev_rim(packs[0], 1)
        from_right = dev_rim(packs[1], -1)
        from_low = grp_rim(packs[2], 1)
        from_high = grp_rim(packs[3], -1)
        extended = jnp.concatenate([state_bf, from_left, from_right, from_low, from_high], axis=0)
        gathered = jnp.dot(
            column_select,
            extended.reshape(ext_count, flat_width),
            preferred_element_type=jnp.float32,
        ).astype(jnp.bfloat16)
        gathered = gathered.reshape(tile_count, stored, vectors_count, tile_rows)
        return jnp.einsum("tkij,tkrj->tri", jacobian, gathered, preferred_element_type=jnp.float32)

    def jacobi(vectors):
        return jnp.einsum(
            "tij,trj->tri",
            smoother,
            vectors.astype(jnp.bfloat16),
            preferred_element_type=jnp.float32,
        )

    position = lax.axis_index("dev")
    mine = lax.dynamic_slice_in_dim(owner[:, 0], position * blocks, blocks)
    order = jnp.arange(blocks, dtype=jnp.int32)
    earlier = (mine[:, None] == mine[None, :]) & (order[None, :] < order[:, None])
    slot = jnp.sum(earlier.astype(jnp.int32), axis=1)
    fetched = lax.all_to_all(coarse_inverse[0], "dev", split_axis=0, concat_axis=0, tiled=True)
    rim_rhs = jnp.dot(
        rim_select, rhs.astype(jnp.bfloat16).reshape(tile_count, flat_width), preferred_element_type=jnp.float32
    ).astype(jnp.bfloat16)
    rim_smoother = jnp.dot(
        rim_select, smoother.reshape(tile_count, tile_rows * tile_rows), preferred_element_type=jnp.float32
    ).astype(jnp.bfloat16)
    first_packs = OMEGA * jnp.einsum(
        "tij,trj->tri",
        rim_smoother.reshape(-1, tile_rows, tile_rows),
        rim_rhs.reshape(-1, vectors_count, tile_rows),
        preferred_element_type=jnp.float32,
    )
    first_packs = first_packs.astype(jnp.bfloat16)
    state = OMEGA * jacobi(rhs)
    for sweep in range(SWEEPS - 1):
        state = state + OMEGA * jacobi(rhs - operate(state, first_packs if sweep == 0 else None))
    residual = rhs - operate(state)
    restricted = jnp.einsum(
        "tij,trj->tri",
        restriction,
        residual.astype(jnp.bfloat16),
        preferred_element_type=jnp.float32,
    )
    partial_sum = restricted.reshape(blocks, AGG, vectors_count, tile_rows).sum(axis=1)
    groups = lax.axis_size("grp")
    group = lax.axis_index("grp")
    share = blocks // groups
    quarters = partial_sum.astype(jnp.bfloat16).reshape(groups, share, vectors_count, tile_rows)
    total = quarters[group].astype(jnp.float32)
    for by in range(1, groups):
        pairs = [(i, (i + by) % groups) for i in range(groups)]
        total = total + lax.ppermute(quarters[(group + by) % groups], "grp", pairs).astype(jnp.float32)
    coarse = total.astype(jnp.bfloat16)
    mine_share = lax.dynamic_slice_in_dim(mine, group * share, share)
    slot_share = lax.dynamic_slice_in_dim(slot, group * share, share)
    picked_share = fetched[mine_share, slot_share]
    solved = jnp.einsum("cab,crb->cra", picked_share, coarse, preferred_element_type=jnp.float32)
    fix_share = solved.astype(jnp.bfloat16)
    pieces = [fix_share]
    for by in range(1, groups):
        pairs = [(i, (i + by) % groups) for i in range(groups)]
        pieces.append(lax.ppermute(fix_share, "grp", pairs))
    stacked = jnp.stack(pieces)
    order = (group - jnp.arange(groups, dtype=jnp.int32)) % groups
    coarse_fix = jnp.take(stacked, order, axis=0).reshape(blocks, vectors_count, tile_rows)
    fine_fix = jnp.repeat(coarse_fix, AGG, axis=0)
    state = state + jnp.einsum(
        "tji,trj->tri", restriction, fine_fix, preferred_element_type=jnp.float32
    )
    for sweep in range(SWEEPS):
        state = state + OMEGA * jacobi(rhs - operate(state))
    return state


def solution(mesh):
    in_specs = (
        P(("grp", "dev"), None, None),
        P(("grp", "dev"), None, None, None),
        P(("grp", "dev"), None),
        P(("grp", "dev"), None, None),
        P(("grp", "dev"), None, None),
        P(("grp", "dev"), None, None),
        P("dev", None, None, None, None),
        P(),
    )
    out_specs = P(("grp", "dev"), None, None)
    return jax.shard_map(shards, mesh=mesh, in_specs=in_specs, out_specs=out_specs, check_vma=False)
```

```python
import jax
import jax.numpy as jnp
from jax import lax
from jax.sharding import PartitionSpec as P

AGG = 2
SWEEPS = 3


OMEGA = 0.8


def shifted(value, axis, by):
    length = lax.axis_size(axis)
    pairs = [(i, i + by) for i in range(length) if 0 <= i + by < length]
    return lax.ppermute(value, axis, pairs)


def dev_rim(pack, offset):
    return shifted(pack, "dev", offset)


def grp_rim(pack, offset):
    return shifted(pack, "grp", offset)


def shards(rhs, jacobian, columns, send_tiles, smoother, restriction, coarse_inverse, owner):
    tile_count = rhs.shape[0]
    vectors_count = rhs.shape[1]
    tile_rows = rhs.shape[2]
    stored = columns.shape[1]
    blocks = tile_count // AGG
    listed = send_tiles[0]
    rim_count = listed.shape[1]
    ext_count = tile_count + 4 * rim_count
    flat_width = vectors_count * tile_rows
    ext_range = jnp.arange(ext_count, dtype=jnp.int32)
    column_select = (columns[:, 1:].reshape(-1)[:, None] == ext_range[None, :]).astype(jnp.bfloat16)
    own_range = jnp.arange(tile_count, dtype=jnp.int32)
    rim_select = (listed.reshape(-1)[:, None] == own_range[None, :]).astype(jnp.bfloat16)

    def operate(state):
        state_bf = state.astype(jnp.bfloat16)
        state_flat = state_bf.reshape(tile_count, flat_width)
        packs = jnp.dot(rim_select, state_flat, preferred_element_type=jnp.float32).astype(
            jnp.bfloat16
        )
        packs = packs.reshape(4, rim_count, vectors_count, tile_rows)
        from_left = dev_rim(packs[0], 1)
        from_right = dev_rim(packs[1], -1)
        from_low = grp_rim(packs[2], 1)
        from_high = grp_rim(packs[3], -1)
        extended = jnp.concatenate([state_bf, from_left, from_right, from_low, from_high], axis=0)
        gathered = jnp.dot(
            column_select,
            extended.reshape(ext_count, flat_width),
            preferred_element_type=jnp.float32,
        ).astype(jnp.bfloat16)
        gathered = gathered.reshape(tile_count, stored - 1, vectors_count, tile_rows)
        gathered = jnp.concatenate([state_bf[:, None], gathered], axis=1)
        return jnp.einsum("tkij,tkrj->tri", jacobian, gathered, preferred_element_type=jnp.float32)

    def jacobi(vectors):
        return jnp.einsum(
            "tij,trj->tri",
            smoother,
            vectors.astype(jnp.bfloat16),
            preferred_element_type=jnp.float32,
        )

    position = lax.axis_index("dev")
    mine = lax.dynamic_slice_in_dim(owner[:, 0], position * blocks, blocks)
    order = jnp.arange(blocks, dtype=jnp.int32)
    earlier = (mine[:, None] == mine[None, :]) & (order[None, :] < order[:, None])
    slot = jnp.sum(earlier.astype(jnp.int32), axis=1)
    fetched = lax.all_to_all(coarse_inverse[0], "dev", split_axis=0, concat_axis=0, tiled=True)
    state = OMEGA * jacobi(rhs)
    for sweep in range(SWEEPS - 1):
        state = state + OMEGA * jacobi(rhs - operate(state))
    residual = rhs - operate(state)
    restricted = jnp.einsum(
        "tij,trj->tri",
        restriction,
        residual.astype(jnp.bfloat16),
        preferred_element_type=jnp.float32,
    )
    partial_sum = restricted.reshape(blocks, AGG, vectors_count, tile_rows).sum(axis=1)
    groups = lax.axis_size("grp")
    group = lax.axis_index("grp")
    share = blocks // groups
    quarters = partial_sum.astype(jnp.bfloat16).reshape(groups, share, vectors_count, tile_rows)
    total = quarters[group].astype(jnp.float32)
    for by in range(1, groups):
        pairs = [(i, (i + by) % groups) for i in range(groups)]
        total = total + lax.ppermute(quarters[(group + by) % groups], "grp", pairs).astype(jnp.float32)
    coarse = total.astype(jnp.bfloat16)
    mine_share = lax.dynamic_slice_in_dim(mine, group * share, share)
    slot_share = lax.dynamic_slice_in_dim(slot, group * share, share)
    picked_share = fetched[mine_share, slot_share]
    solved = jnp.einsum("cab,crb->cra", picked_share, coarse, preferred_element_type=jnp.float32)
    fix_share = solved.astype(jnp.bfloat16)
    pieces = [fix_share]
    for by in range(1, groups):
        pairs = [(i, (i + by) % groups) for i in range(groups)]
        pieces.append(lax.ppermute(fix_share, "grp", pairs))
    stacked = jnp.stack(pieces)
    order = (group - jnp.arange(groups, dtype=jnp.int32)) % groups
    coarse_fix = jnp.take(stacked, order, axis=0).reshape(blocks, vectors_count, tile_rows)
    fine_fix = jnp.repeat(coarse_fix, AGG, axis=0)
    state = state + jnp.einsum(
        "tji,trj->tri", restriction, fine_fix, preferred_element_type=jnp.float32
    )
    for sweep in range(SWEEPS):
        state = state + OMEGA * jacobi(rhs - operate(state))
    return state


def solution(mesh):
    in_specs = (
        P(("grp", "dev"), None, None),
        P(("grp", "dev"), None, None, None),
        P(("grp", "dev"), None),
        P(("grp", "dev"), None, None),
        P(("grp", "dev"), None, None),
        P(("grp", "dev"), None, None),
        P("dev", None, None, None, None),
        P(),
    )
    out_specs = P(("grp", "dev"), None, None)
    return jax.shard_map(shards, mesh=mesh, in_specs=in_specs, out_specs=out_specs, check_vma=False)
```

```python
import jax
import jax.numpy as jnp
from jax import lax
from jax.sharding import PartitionSpec as P

AGG = 2
SWEEPS = 3


OMEGA = 0.8


def shifted(value, axis, by):
    length = lax.axis_size(axis)
    pairs = [(i, i + by) for i in range(length) if 0 <= i + by < length]
    return lax.ppermute(value, axis, pairs)


def dev_rim(pack, offset):
    return shifted(pack, "dev", offset)


def grp_rim(pack, offset):
    return shifted(pack, "grp", offset)


def shards(rhs, jacobian, columns, send_tiles, smoother, restriction, coarse_inverse, owner):
    tile_count = rhs.shape[0]
    vectors_count = rhs.shape[1]
    tile_rows = rhs.shape[2]
    stored = columns.shape[1]
    blocks = tile_count // AGG
    listed = send_tiles[0]
    rim_count = listed.shape[1]
    ext_count = tile_count + 4 * rim_count
    flat_width = vectors_count * tile_rows
    ext_range = jnp.arange(ext_count, dtype=jnp.int32)
    column_select = (columns.reshape(-1)[:, None] == ext_range[None, :]).astype(jnp.bfloat16)
    own_range = jnp.arange(tile_count, dtype=jnp.int32)
    rim_select = (listed.reshape(-1)[:, None] == own_range[None, :]).astype(jnp.bfloat16)

    def operate(state):
        state_bf = state.astype(jnp.bfloat16)
        state_flat = state_bf.reshape(tile_count, flat_width)
        packs = jnp.dot(rim_select, state_flat, preferred_element_type=jnp.float32).astype(
            jnp.bfloat16
        )
        packs = packs.reshape(4, rim_count, vectors_count, tile_rows)
        from_left = dev_rim(packs[0], 1)
        from_right = dev_rim(packs[1], -1)
        from_low = grp_rim(packs[2], 1)
        from_high = grp_rim(packs[3], -1)
        extended = jnp.concatenate([state_bf, from_left, from_right, from_low, from_high], axis=0)
        gathered = jnp.dot(
            column_select,
            extended.reshape(ext_count, flat_width),
            preferred_element_type=jnp.float32,
        ).astype(jnp.bfloat16)
        gathered = gathered.reshape(tile_count, stored, vectors_count, tile_rows)
        return jnp.einsum("tkij,tkrj->tri", jacobian, gathered, preferred_element_type=jnp.float32)

    def jacobi(vectors):
        return jnp.einsum(
            "tij,trj->tri",
            smoother,
            vectors.astype(jnp.bfloat16),
            preferred_element_type=jnp.float32,
        )

    position = lax.axis_index("dev")
    mine = lax.dynamic_slice_in_dim(owner[:, 0], position * blocks, blocks)
    order = jnp.arange(blocks, dtype=jnp.int32)
    earlier = (mine[:, None] == mine[None, :]) & (order[None, :] < order[:, None])
    slot = jnp.sum(earlier.astype(jnp.int32), axis=1)
    fetched = lax.all_to_all(coarse_inverse[0], "dev", split_axis=0, concat_axis=0, tiled=True)
    state = OMEGA * jacobi(rhs)
    for sweep in range(SWEEPS - 1):
        state = state + OMEGA * jacobi(rhs - operate(state))
    residual = rhs - operate(state)
    restricted = jnp.einsum(
        "tij,trj->tri",
        restriction,
        residual.astype(jnp.bfloat16),
        preferred_element_type=jnp.float32,
    )
    partial_sum = restricted.reshape(blocks, AGG, vectors_count, tile_rows).sum(axis=1)
    groups = lax.axis_size("grp")
    group = lax.axis_index("grp")
    share = blocks // groups
    quarters = partial_sum.astype(jnp.bfloat16).reshape(groups, share, vectors_count, tile_rows)
    total = quarters[group].astype(jnp.float32)
    for by in range(1, groups):
        pairs = [(i, (i + by) % groups) for i in range(groups)]
        total = total + lax.ppermute(quarters[(group + by) % groups], "grp", pairs).astype(jnp.float32)
    coarse = total.astype(jnp.bfloat16)
    mine_share = lax.dynamic_slice_in_dim(mine, group * share, share)
    slot_share = lax.dynamic_slice_in_dim(slot, group * share, share)
    picked_share = fetched[mine_share, slot_share]
    solved = jnp.einsum("cab,crb->cra", picked_share, coarse, preferred_element_type=jnp.float32)
    fix_share = solved.astype(jnp.bfloat16)
    pieces = [fix_share]
    for by in range(1, groups):
        pairs = [(i, (i + by) % groups) for i in range(groups)]
        pieces.append(lax.ppermute(fix_share, "grp", pairs))
    span = tile_count // groups
    updated = state
    for by, piece in enumerate(pieces):
        start = ((group - by) % groups) * span
        fine_fix = jnp.repeat(piece, AGG, axis=0)
        lifted = lax.dynamic_slice_in_dim(state, start, span) + jnp.einsum(
            "tji,trj->tri",
            lax.dynamic_slice_in_dim(restriction, start, span),
            fine_fix,
            preferred_element_type=jnp.float32,
        )
        updated = lax.dynamic_update_slice_in_dim(updated, lifted, start, 0)
    state = updated
    for sweep in range(SWEEPS):
        state = state + OMEGA * jacobi(rhs - operate(state))
    return state


def solution(mesh):
    in_specs = (
        P(("grp", "dev"), None, None),
        P(("grp", "dev"), None, None, None),
        P(("grp", "dev"), None),
        P(("grp", "dev"), None, None),
        P(("grp", "dev"), None, None),
        P(("grp", "dev"), None, None),
        P("dev", None, None, None, None),
        P(),
    )
    out_specs = P(("grp", "dev"), None, None)
    return jax.shard_map(shards, mesh=mesh, in_specs=in_specs, out_specs=out_specs, check_vma=False)
```

```python
import jax
import jax.numpy as jnp
from jax import lax
from jax.sharding import PartitionSpec as P

AGG = 2
SWEEPS = 3


OMEGA = 0.8


def shifted(value, axis, by):
    length = lax.axis_size(axis)
    pairs = [(i, i + by) for i in range(length) if 0 <= i + by < length]
    return lax.ppermute(value, axis, pairs)


def dev_rim(pack, offset):
    return shifted(pack, "dev", offset)


def grp_rim(pack, offset):
    return shifted(pack, "grp", offset)


def shards(rhs, jacobian, columns, send_tiles, smoother, restriction, coarse_inverse, owner):
    tile_count = rhs.shape[0]
    vectors_count = rhs.shape[1]
    tile_rows = rhs.shape[2]
    stored = columns.shape[1]
    blocks = tile_count // AGG
    listed = send_tiles[0]
    rim_count = listed.shape[1]
    ext_count = tile_count + 4 * rim_count
    flat_width = vectors_count * tile_rows
    ext_range = jnp.arange(ext_count, dtype=jnp.int32)
    column_select = (columns.reshape(-1)[:, None] == ext_range[None, :]).astype(jnp.bfloat16)
    own_range = jnp.arange(tile_count, dtype=jnp.int32)
    rim_select = (listed.reshape(-1)[:, None] == own_range[None, :]).astype(jnp.bfloat16)

    def operate(state):
        state_bf = state.astype(jnp.bfloat16)
        state_flat = state_bf.reshape(tile_count, flat_width)
        packs = jnp.dot(rim_select, state_flat, preferred_element_type=jnp.float32).astype(
            jnp.bfloat16
        )
        packs = packs.reshape(4, rim_count, vectors_count, tile_rows)
        from_left = dev_rim(packs[0], 1)
        from_right = dev_rim(packs[1], -1)
        from_low = grp_rim(packs[2], 1)
        from_high = grp_rim(packs[3], -1)
        extended = jnp.concatenate([state_bf, from_left, from_right, from_low, from_high], axis=0)
        gathered = jnp.dot(
            column_select,
            extended.reshape(ext_count, flat_width),
            preferred_element_type=jnp.float32,
        ).astype(jnp.bfloat16)
        gathered = gathered.reshape(tile_count, stored, vectors_count, tile_rows)
        return jnp.einsum("tkij,tkrj->tri", jacobian, gathered, preferred_element_type=jnp.float32)

    def jacobi(vectors):
        return jnp.einsum(
            "tij,trj->tri",
            smoother,
            vectors.astype(jnp.bfloat16),
            preferred_element_type=jnp.float32,
        )

    position = lax.axis_index("dev")
    mine = lax.dynamic_slice_in_dim(owner[:, 0], position * blocks, blocks)
    order = jnp.arange(blocks, dtype=jnp.int32)
    earlier = (mine[:, None] == mine[None, :]) & (order[None, :] < order[:, None])
    slot = jnp.sum(earlier.astype(jnp.int32), axis=1)
    fetched = lax.all_to_all(coarse_inverse[0], "dev", split_axis=0, concat_axis=0, tiled=True)
    state = OMEGA * jacobi(rhs)
    for sweep in range(SWEEPS - 1):
        state = state + OMEGA * jacobi(rhs - operate(state))
    residual = rhs - operate(state)
    restricted = jnp.einsum(
        "tij,trj->tri",
        restriction,
        residual.astype(jnp.bfloat16),
        preferred_element_type=jnp.float32,
    )
    partial_sum = restricted.reshape(blocks, AGG, vectors_count, tile_rows).sum(axis=1)
    groups = lax.axis_size("grp")
    group = lax.axis_index("grp")
    share = blocks // groups
    quarters = partial_sum.astype(jnp.bfloat16).reshape(groups, share, vectors_count, tile_rows)
    total = quarters[group].astype(jnp.float32)
    for by in range(1, groups):
        pairs = [(i, (i + by) % groups) for i in range(groups)]
        total = total + lax.ppermute(quarters[(group + by) % groups], "grp", pairs).astype(jnp.float32)
    coarse = total.astype(jnp.bfloat16)
    mine_share = lax.dynamic_slice_in_dim(mine, group * share, share)
    slot_share = lax.dynamic_slice_in_dim(slot, group * share, share)
    picked_share = fetched[mine_share, slot_share]
    solved = jnp.einsum("cab,crb->cra", picked_share, coarse, preferred_element_type=jnp.float32)
    fix_share = solved.astype(jnp.bfloat16)
    pieces = [fix_share]
    for by in range(1, groups):
        pairs = [(i, (i + by) % groups) for i in range(groups)]
        pieces.append(lax.ppermute(fix_share, "grp", pairs))
    doubled = jnp.stack(pieces[::-1] + pieces[::-1])
    coarse_fix = lax.dynamic_slice_in_dim(doubled, groups - 1 - group, groups).reshape(blocks, vectors_count, tile_rows)
    fine_fix = jnp.repeat(coarse_fix, AGG, axis=0)
    state = state + jnp.einsum(
        "tji,trj->tri", restriction, fine_fix, preferred_element_type=jnp.float32
    )
    for sweep in range(SWEEPS):
        state = state + OMEGA * jacobi(rhs - operate(state))
    return state


def solution(mesh):
    in_specs = (
        P(("grp", "dev"), None, None),
        P(("grp", "dev"), None, None, None),
        P(("grp", "dev"), None),
        P(("grp", "dev"), None, None),
        P(("grp", "dev"), None, None),
        P(("grp", "dev"), None, None),
        P("dev", None, None, None, None),
        P(),
    )
    out_specs = P(("grp", "dev"), None, None)
    return jax.shard_map(shards, mesh=mesh, in_specs=in_specs, out_specs=out_specs, check_vma=False)
```
